32 devices in a mesh: dp: 4 (over y, x), expert: 8 (over z, core).
Axes of the slice: x: 2, y: 2, z: 4, core: 2. Of those that a mesh axis runs over, the one named last changes fastest.
Arguments:
- context: bfloat16 [8, 4, 128, 1536], P('expert', None, None, 'dp'), may hold values from -0.29882812 to 0.29882812
- w_proj: bfloat16 [1536, 1536], P('dp'), may hold values from -0.15625 to 0.15625
- residual: bfloat16 [4096, 1536], P(('dp', 'expert')), may hold values from -0.29882812 to 0.29882812
- gain_first: float32 [1536], replicated, may hold values from 0.25 to 1.75
- gain_next: float32 [1536], replicated, may hold values from 0.25 to 1.75
- w_router: bfloat16 [1536, 40], replicated, may hold values from -0.15625 to 0.15625
- expert_ids: int32 [4096, 8], P(('dp', 'expert')), may hold values from 0 to 39, all different within a row
- replica_pick: int32 [4096, 8], P(('dp', 'expert')), may hold values from 0 to 5039
- slot_expert: int32 [48], replicated, may hold values from 0 to 39, as said below
- cap_blocks: int32 [48], replicated, may hold values from 1 to 4
- w_in: bfloat16 [48, 1536, 1024], P('expert', 'dp'), as said below
- w_out: bfloat16 [48, 512, 1536], P('expert', 'dp'), as said below
Outputs:
- residual_out: bfloat16 [4096, 1536], P(('dp', 'expert'))
- next_normed: bfloat16 [4096, 1536], P(('dp', 'expert'))
The draws below stay inside these ranges and needn't reach their ends.
Inputs may be any that keep to these rules, and one draw needn't show every extreme that they name: `slot_expert`: every expert is held by at least one slot; slot s lies on index s // 6 of the expert axis. `w_in`: two slots that hold the same expert have equal weights. `w_out`: two slots that hold the same expert have equal weights.
All inputs are finite; a program needn't handle non-finite values.
Results may differ from the reference program's by a relative error of at most 0.01.
Values may be sent and summed in bfloat16 or wider, within the bound.
No kernel may reach another device: no remote copies, remote signals or barrier semaphores. Data moves between devices by JAX's collectives and lax.ppermute only.
A program may use at most 128 MiB of HBM per device.

```python
import jax
import jax.numpy as jnp
from jax import lax

D = 1536
FF = 512
EXPERTS = 40
TOPK = 8
TOK_DEV = 128
BLOCKS_MOST = 4
CAP_UNIT = 8
CAP_MOST = 32
SLOTS = 48
TOKENS = 4096
N_DP = 4
N_EXPERT = 8


def placement_table(key):
    extra = jax.random.randint(jax.random.fold_in(key, 11), (SLOTS - EXPERTS,), 0, EXPERTS).astype(jnp.int32)
    table = jnp.concatenate([jnp.arange(EXPERTS).astype(jnp.int32), extra])
    order = jax.random.permutation(jax.random.fold_in(key, 12), SLOTS)
    return table[order]


def draw_slot_expert(key, part):
    return placement_table(key)


def draw_w_in(key, part):
    table = placement_table(key)
    experts_all = jax.random.normal(jax.random.fold_in(key, 21), (EXPERTS, D, 2 * FF), jnp.float32) * D ** (-0.5)
    return experts_all[table].astype(jnp.bfloat16)


def draw_w_out(key, part):
    table = placement_table(key)
    experts_all = jax.random.normal(jax.random.fold_in(key, 22), (EXPERTS, FF, D), jnp.float32) * FF ** (-0.5)
    return experts_all[table].astype(jnp.bfloat16)


def place_ends(values, stream_key, low, high):
    place = [jax.random.randint(jax.random.fold_in(stream_key, axis), (), 0, length) for axis, length in enumerate(values.shape)]
    main_axis = values.shape.index(max(values.shape))
    next_to = place[:main_axis] + [(place[main_axis] + 1) % values.shape[main_axis]] + place[main_axis + 1:]
    return values.at[tuple(place)].set(low).at[tuple(next_to)].set(high)


def strengthened(values, rng, source, target, blocks, factor):
    owner, partner = [(jnp.arange(values.shape[dim]) // (values.shape[dim] // blocks)).reshape([-1 if axis == dim else 1 for axis in range(values.ndim)]) for dim in (source, target)]
    chosen = jax.random.permutation(rng, blocks)[partner]
    strong = (owner == chosen) | (owner == (partner + blocks // 2) % blocks)
    return jnp.where(strong, factor * values, values)


def block_scale(key, dims, pieces, low, largest):
    level, own = 1.0, jax.random.fold_in(key, 6)
    for axis_at, blocks in pieces:
        steps = jnp.exp(jax.random.uniform(jax.random.fold_in(own, axis_at), (blocks,), jnp.float32, low / len(pieces), largest / len(pieces)))
        level = level * jnp.repeat(steps, dims[axis_at] // blocks).reshape([-1 if axis == axis_at else 1 for axis in range(len(dims))])
    return level


def picks_of(key, rows, number_of, top, lift):
    ranking = jax.random.permutation(jax.random.fold_in(key, 1), number_of)
    favour = ranking
    for power in range(3):
        favour = favour * favour // number_of
    favour = favour * lift // number_of
    tickets = jax.random.randint(jax.random.fold_in(key, 2), (rows, number_of), 0, 4096) + favour
    holders = jax.random.permutation(jax.random.fold_in(key, 3), rows)[jnp.arange(number_of) % rows]
    tickets = jnp.where(jnp.arange(rows)[:, None] == holders[None, :], 1 << 14, tickets)
    score = tickets * number_of + jnp.arange(number_of)
    return lax.top_k(score.astype(jnp.int32), top)[1].astype(jnp.int32)


def noise(own_key, dims, width, most, split=(), kind=jnp.bfloat16):
    values = width * jax.random.normal(own_key, dims, jnp.float32)
    if split:
        values = values * block_scale(own_key, dims, split, -0.22, 0.18)
    return jnp.clip(values, -most, most).astype(kind)


def heavy_noise(stream_key, extent, spread, reach, cuts, heavy, held_as=jnp.bfloat16):
    drawn = spread * jax.random.normal(stream_key, extent, jnp.float32)
    if cuts:
        drawn = drawn * block_scale(stream_key, extent, cuts, -0.22, 0.18)
    return jnp.clip(strengthened(drawn, jax.random.fold_in(stream_key, 3), *heavy), -reach, reach).astype(held_as)


def setup_inputs(seed: int = 0) -> dict:
    splits = jax.random.split(jax.random.key(seed), 13)
    context = heavy_noise(splits[0], (N_EXPERT, N_DP, TOK_DEV, D), 0.05, 0.29882812, ((0, 8), (3, 4)), (3, 1, 4, 2.0))
    w_proj = noise(splits[1], (D, D), D ** -0.5, 0.15625, ((0, 4),))
    residual = noise(splits[2], (TOKENS, D), 0.05, 0.29882812, ((0, 32),))
    gain_first = jnp.clip(1.0 + 0.15 * jax.random.normal(splits[3], (D,), jnp.float32), 0.25, 1.75)
    gain_next = jnp.clip(1.0 + 0.15 * jax.random.normal(splits[4], (D,), jnp.float32), 0.25, 1.75)
    w_router = noise(splits[5], (D, EXPERTS), D ** -0.5, 0.15625)
    expert_ids = picks_of(splits[6], TOKENS, EXPERTS, TOPK, 3276)
    replica_pick = place_ends(jax.random.randint(splits[7], (TOKENS, TOPK), 0, 5040), jax.random.fold_in(splits[7], 1), 0, 5039).astype(jnp.int32)
    slot_expert = draw_slot_expert(jax.random.fold_in(splits[12], 71), 0)
    cap_blocks = place_ends(jax.random.randint(splits[9], (SLOTS,), 1, BLOCKS_MOST + 1), jax.random.fold_in(splits[9], 1), 1, BLOCKS_MOST).astype(jnp.int32)
    w_in = draw_w_in(jax.random.fold_in(splits[12], 71), 0)
    w_out = draw_w_out(jax.random.fold_in(splits[12], 71), 0)
    return dict(context=context, w_proj=w_proj, residual=residual, gain_first=gain_first, gain_next=gain_next, w_router=w_router, expert_ids=expert_ids, replica_pick=replica_pick, slot_expert=slot_expert, cap_blocks=cap_blocks, w_in=w_in, w_out=w_out)


def rms_scale(values, gain):
    widened = values.astype(jnp.float32)
    return widened * lax.rsqrt(lax.optimization_barrier(jnp.mean(widened * widened, axis=-1, keepdims=True)) + 1e-06) * gain

def route_rows(normed, w_router, expert_ids, replica_pick, slot_expert, cap_blocks, groups, cap_unit):
    row_count = normed.shape[0]
    experts_all = w_router.shape[1]
    slots_all = slot_expert.shape[0]
    topk_all = expert_ids.shape[1]
    logits = jnp.dot(normed, w_router, preferred_element_type=jnp.float32)
    expert_axis = jnp.arange(experts_all).astype(jnp.int32)
    one_hot = expert_ids[:, :, None] == expert_axis
    chosen = lax.optimization_barrier(jnp.sum(jnp.where(one_hot, logits[:, None, :], jnp.float32(0.0)), axis=-1))
    raised = jnp.exp(chosen)
    gates = raised / lax.optimization_barrier(jnp.sum(raised, axis=-1, keepdims=True))
    holder = (slot_expert[None, :] == expert_axis[:, None]).astype(jnp.int32)
    rep_count = lax.optimization_barrier(jnp.sum(holder, axis=1)).astype(jnp.int32)
    earlier = (jnp.cumsum(holder, axis=1).astype(jnp.int32) - holder).astype(jnp.int32)
    slot_rank = lax.optimization_barrier(jnp.sum(earlier * holder, axis=0)).astype(jnp.int32)
    count_of = lax.optimization_barrier(jnp.sum(jnp.where(one_hot, rep_count, 0), axis=-1)).astype(jnp.int32)
    replica = (replica_pick % count_of).astype(jnp.int32)
    slot_axis = jnp.arange(slots_all).astype(jnp.int32)
    matched = (slot_expert == expert_ids[:, :, None]) & (slot_rank == replica[:, :, None])
    target_slot = lax.optimization_barrier(jnp.sum(jnp.where(matched, slot_axis, 0), axis=-1)).astype(jnp.int32)
    selected = matched.astype(jnp.int32).reshape(groups, -1, slots_all)
    before = (jnp.cumsum(selected, axis=1).astype(jnp.int32) - selected).astype(jnp.int32)
    position = lax.optimization_barrier(jnp.sum(before * selected, axis=-1)).astype(jnp.int32).reshape(row_count, topk_all)
    capacity = lax.optimization_barrier(jnp.sum(jnp.where(target_slot[:, :, None] == slot_axis, cap_blocks, 0), axis=-1)).astype(jnp.int32) * cap_unit
    retained = position < capacity
    return (gates, target_slot, position, retained)

def reference(context, w_proj, residual, gain_first, gain_next, w_router, expert_ids, replica_pick, slot_expert, cap_blocks, w_in, w_out):
    devices_all = N_DP * N_EXPERT
    context_rows = jnp.transpose(context, (1, 0, 2, 3)).reshape(TOKENS, D)
    attended = jnp.dot(context_rows, w_proj, preferred_element_type=jnp.float32)
    hidden_state = (residual.astype(jnp.float32) + attended).astype(jnp.bfloat16)
    normed = rms_scale(hidden_state, gain_first).astype(jnp.bfloat16)
    gates, target_slot, position, retained = route_rows(normed, w_router, expert_ids, replica_pick, slot_expert, cap_blocks, devices_all, CAP_UNIT)
    flat_total = TOKENS * TOPK
    device_of = jnp.broadcast_to((jnp.arange(TOKENS) // TOK_DEV).astype(jnp.int32)[:, None], (TOKENS, TOPK))
    target = jnp.where(retained, position, CAP_MOST).astype(jnp.int32)
    flat_ids = jnp.arange(flat_total).astype(jnp.int32).reshape(TOKENS, TOPK)
    index_table = jnp.full((SLOTS, devices_all, CAP_MOST), flat_total, jnp.int32)
    index_table = index_table.at[target_slot, device_of, target].set(flat_ids, mode='drop')
    flat_gates = gates.reshape(-1)

    def expert_step(combined, inputs):
        table_slot, slot_in, slot_out = inputs
        slot_ids = table_slot.reshape(-1)
        valid = slot_ids < flat_total
        clipped = jnp.minimum(slot_ids, flat_total - 1).astype(jnp.int32)
        token_index = (clipped // TOPK).astype(jnp.int32)
        gathered = normed[token_index]
        gate_up = jnp.dot(gathered, slot_in, preferred_element_type=jnp.float32)
        activated = (jax.nn.silu(gate_up[:, :FF]) * gate_up[:, FF:]).astype(jnp.bfloat16)
        expert_out = jnp.dot(activated, slot_out, preferred_element_type=jnp.float32).astype(jnp.bfloat16)
        weighting = jnp.where(valid, flat_gates[clipped], jnp.float32(0.0))
        combined = combined.at[token_index].add(expert_out.astype(jnp.float32) * weighting[:, None])
        return (combined, None)
    combined, _ = lax.scan(expert_step, jnp.zeros((TOKENS, D), jnp.float32), (index_table, w_in, w_out))
    residual_out = (hidden_state.astype(jnp.float32) + combined).astype(jnp.bfloat16)
    next_normed = rms_scale(residual_out, gain_next).astype(jnp.bfloat16)
    return (residual_out, next_normed)
```

```python
import math

import jax
import jax.numpy as jnp
from jax import lax
from jax.sharding import PartitionSpec as P

CAP_UNIT = 8
CAP_MOST = 32


def rms_scale(values, gain):
    widened = values.astype(jnp.float32)
    return widened * lax.rsqrt(jnp.mean(widened * widened, axis=-1, keepdims=True) + 1e-06) * gain


def route_rows(normed, w_router, expert_ids, replica_pick, slot_expert, cap_blocks, cap_unit):
    row_count, topk_all = expert_ids.shape
    experts_all = w_router.shape[1]
    slots_all = slot_expert.shape[0]
    logits = jnp.dot(normed, w_router, preferred_element_type=jnp.float32)
    expert_axis = jnp.arange(experts_all)
    one_hot = expert_ids[:, :, None] == expert_axis
    chosen = jnp.sum(jnp.where(one_hot, logits[:, None, :], jnp.float32(0.0)), axis=-1)
    raised = jnp.exp(chosen)
    gates = raised / jnp.sum(raised, axis=-1, keepdims=True)
    holder = (slot_expert[None, :] == expert_axis[:, None]).astype(jnp.int32)
    rep_count = jnp.sum(holder, axis=1)
    earlier = jnp.cumsum(holder, axis=1) - holder
    slot_rank = jnp.sum(earlier * holder, axis=0)
    count_of = jnp.sum(jnp.where(one_hot, rep_count, 0), axis=-1)
    replica = replica_pick % count_of
    slot_axis = jnp.arange(slots_all)
    matched = (slot_expert == expert_ids[:, :, None]) & (slot_rank == replica[:, :, None])
    target_slot = jnp.sum(jnp.where(matched, slot_axis, 0), axis=-1)
    flat_count = row_count * topk_all
    selected = matched.reshape(flat_count, slots_all)
    flat_axis = lax.optimization_barrier(jnp.arange(flat_count))
    lower = (flat_axis[:, None] > flat_axis[None, :]).astype(jnp.bfloat16)
    before = jnp.dot(lower, selected.astype(jnp.bfloat16), preferred_element_type=jnp.float32)
    position = (
        jnp.sum(jnp.where(selected, before, jnp.float32(0.0)), axis=-1)
        .astype(jnp.int32)
        .reshape(row_count, topk_all)
    )
    capacity = (
        jnp.sum(jnp.where(target_slot[:, :, None] == slot_axis, cap_blocks, 0), axis=-1) * cap_unit
    )
    retained = position < capacity
    return (gates, target_slot, position, retained)


def unit_plan(slot_local, n_dp, hidden_units):
    chunks = n_dp // math.gcd(slot_local, n_dp)
    units_per = slot_local * chunks // n_dp
    chunk_width = hidden_units // chunks
    owned = [[((o * units_per + i) // chunks, (o * units_per + i) % chunks) for i in range(units_per)]
             for o in range(n_dp)]
    first_slot = [owned[o][0][0] for o in range(n_dp)]
    slots_per = max(owned[o][-1][0] - first_slot[o] + 1 for o in range(n_dp))
    return chunks, units_per, chunk_width, owned, first_slot, slots_per


def on_device(
    context,
    w_proj,
    residual,
    gain_first,
    gain_next,
    w_router,
    expert_ids,
    replica_pick,
    slot_expert,
    cap_blocks,
    w_in,
    w_out,
):
    tok_rows, model_width = residual.shape
    topk_all = expert_ids.shape[1]
    slot_local, d_local, _ = w_in.shape
    hidden_units = w_in.shape[2] // 2
    ff_local = w_out.shape[1]
    n_dp = lax.axis_size("dp")
    n_exp = lax.axis_size("expert")
    dp_at = lax.axis_index("dp")
    exp_at = lax.axis_index("expert")
    chunks, units_per, chunk_width, owned, first_slot, slots_per = unit_plan(
        slot_local, n_dp, hidden_units
    )
    sources_per_chunk = chunk_width // ff_local
    slot_rows = n_exp * CAP_MOST
    hub_rows = slot_local * slot_rows

    win_parts, wout_parts = [], []
    for o in range(n_dp):
        win_units, wout_units = [], []
        for s, c in owned[o]:
            lo = c * chunk_width
            win_units.append(
                jnp.concatenate(
                    [w_in[s, :, lo:lo + chunk_width],
                     w_in[s, :, hidden_units + lo:hidden_units + lo + chunk_width]],
                    axis=-1,
                )
            )
            wout_units.append(w_out[s])
        win_parts.append(jnp.stack(win_units))
        wout_parts.append(jnp.stack(wout_units))
    win_recv = lax.all_to_all(jnp.stack(win_parts), "dp", 0, 0, tiled=True)
    wout_recv = lax.all_to_all(jnp.stack(wout_parts), "dp", 0, 0, tiled=True)
    unit_in = win_recv.transpose(1, 0, 2, 3).reshape(units_per, n_dp * d_local, 2 * chunk_width)

    flat_context = context.reshape(-1, context.shape[3])
    attended = lax.psum_scatter(
        jnp.dot(flat_context, w_proj, preferred_element_type=jnp.float32),
        "dp",
        scatter_dimension=0,
        tiled=True,
    )
    hidden_state = (residual.astype(jnp.float32) + attended).astype(jnp.bfloat16)
    normed = rms_scale(hidden_state, gain_first).astype(jnp.bfloat16)
    gates, target_slot, position, retained = route_rows(
        normed, w_router, expert_ids, replica_pick, slot_expert, cap_blocks, CAP_UNIT
    )
    dest = target_slot // slot_local
    row_in_hub = (target_slot % slot_local) * slot_rows + exp_at * CAP_MOST + position
    code = jnp.where(retained, dest * hub_rows + row_in_hub, -1).astype(jnp.int32)
    kept_gates = jnp.where(retained, gates, jnp.float32(0.0))

    normed_all = lax.all_gather(normed, "expert", axis=0, tiled=True)
    code_all = lax.all_gather(code, "expert", axis=0, tiled=True)
    gates_all = lax.all_gather(kept_gates, "expert", axis=0, tiled=True)
    local = code_all - exp_at * hub_rows
    valid = (code_all >= 0) & (local >= 0) & (local < hub_rows)
    local = jnp.where(valid, local, -1)
    hit = local[:, :, None] == jnp.arange(hub_rows)
    pick = jnp.any(hit, axis=1).astype(jnp.bfloat16)
    weight = jnp.sum(jnp.where(hit, gates_all[:, :, None], jnp.float32(0.0)), axis=1)
    slot_in = lax.dot_general(
        pick, normed_all, (((0,), (0,)), ((), ())), preferred_element_type=jnp.float32
    ).astype(jnp.bfloat16)
    slot_in = slot_in.reshape(slot_local, slot_rows, model_width)

    x_parts = []
    for o in range(n_dp):
        x_parts.append(
            jnp.stack([slot_in[min(first_slot[o] + j, slot_local - 1)] for j in range(slots_per)])
        )
    x_recv = lax.all_to_all(jnp.stack(x_parts), "dp", 0, 0, tiled=True)

    unit_rows = n_dp * slot_rows
    y_acc = jnp.zeros((slots_per, unit_rows, model_width), jnp.float32)
    my_first = (dp_at * units_per) // chunks
    for i in range(units_per):
        unit = dp_at * units_per + i
        slot_at = unit // chunks - my_first
        chunk_at = unit % chunks
        rows = lax.dynamic_index_in_dim(x_recv, slot_at, axis=1, keepdims=False)
        rows = rows.reshape(unit_rows, model_width)
        w_down = lax.dynamic_slice_in_dim(
            wout_recv[:, i], chunk_at * sources_per_chunk, sources_per_chunk, axis=0
        ).reshape(chunk_width, model_width)
        gate_up = jnp.dot(rows, unit_in[i], preferred_element_type=jnp.float32)
        activated = (
            jax.nn.silu(gate_up[:, :chunk_width]) * gate_up[:, chunk_width:]
        ).astype(jnp.bfloat16)
        out = jnp.dot(activated, w_down, preferred_element_type=jnp.float32)
        prev = lax.dynamic_index_in_dim(y_acc, slot_at, axis=0, keepdims=False)
        y_acc = lax.dynamic_update_index_in_dim(y_acc, prev + out, slot_at, axis=0)

    y_send = (
        y_acc.reshape(slots_per, n_dp, slot_rows, model_width)
        .transpose(1, 0, 2, 3)
        .astype(jnp.bfloat16)
    )
    y_recv = lax.all_to_all(y_send, "dp", 0, 0, tiled=True)
    slot_out = [None] * slot_local
    for o in range(n_dp):
        mine = {s for s, _ in owned[o]}
        for j in range(slots_per):
            s = first_slot[o] + j
            if s < slot_local and s in mine:
                part = y_recv[o, j].astype(jnp.float32)
                slot_out[s] = part if slot_out[s] is None else slot_out[s] + part
    expert_out = jnp.concatenate(slot_out, axis=0).astype(jnp.bfloat16)

    weight_hi = weight.astype(jnp.bfloat16)
    weight_lo = (weight - weight_hi.astype(jnp.float32)).astype(jnp.bfloat16)
    partial = jnp.dot(weight_hi, expert_out, preferred_element_type=jnp.float32) + jnp.dot(
        weight_lo, expert_out, preferred_element_type=jnp.float32
    )
    combined = lax.psum_scatter(partial, "expert", scatter_dimension=0, tiled=True)
    residual_out = (hidden_state.astype(jnp.float32) + combined).astype(jnp.bfloat16)
    next_normed = rms_scale(residual_out, gain_next).astype(jnp.bfloat16)
    return (residual_out, next_normed)


def solution(mesh):
    placed = (
        P("expert", None, None, "dp"),
        P("dp", None),
        P(("dp", "expert"), None),
        P(),
        P(),
        P(),
        P(("dp", "expert"), None),
        P(("dp", "expert"), None),
        P(),
        P(),
        P("expert", "dp", None),
        P("expert", "dp", None),
    )
    return jax.shard_map(
        on_device,
        mesh=mesh,
        in_specs=placed,
        out_specs=(P(("dp", "expert"), None), P(("dp", "expert"), None)),
        check_vma=False,
    )
```

```python
import math

import jax
import jax.numpy as jnp
from jax import lax
from jax.sharding import PartitionSpec as P

CAP_UNIT = 8
CAP_MOST = 32


def rms_scale(values, gain):
    widened = values.astype(jnp.float32)
    return widened * lax.rsqrt(jnp.mean(widened * widened, axis=-1, keepdims=True) + 1e-06) * gain


def route_rows(normed, w_router, expert_ids, replica_pick, slot_expert, cap_blocks, cap_unit):
    blocks, row_count, topk_all = expert_ids.shape
    experts_all = w_router.shape[1]
    slots_all = slot_expert.shape[0]
    logits = jnp.dot(normed, w_router, preferred_element_type=jnp.float32)
    logits = logits.reshape(blocks, row_count, experts_all)
    expert_axis = jnp.arange(experts_all)
    one_hot = expert_ids[..., None] == expert_axis
    chosen = jnp.sum(jnp.where(one_hot, logits[:, :, None, :], jnp.float32(0.0)), axis=-1)
    raised = jnp.exp(chosen)
    gates = raised / jnp.sum(raised, axis=-1, keepdims=True)
    holder = (slot_expert[None, :] == expert_axis[:, None]).astype(jnp.int32)
    rep_count = jnp.sum(holder, axis=1)
    earlier = jnp.cumsum(holder, axis=1) - holder
    slot_rank = jnp.sum(earlier * holder, axis=0)
    count_of = jnp.sum(jnp.where(one_hot, rep_count, 0), axis=-1)
    replica = replica_pick % count_of
    slot_axis = jnp.arange(slots_all)
    matched = (slot_expert == expert_ids[..., None]) & (slot_rank == replica[..., None])
    target_slot = jnp.sum(jnp.where(matched, slot_axis, 0), axis=-1)
    flat_count = row_count * topk_all
    selected = matched.reshape(blocks, flat_count, slots_all)
    flat_axis = lax.optimization_barrier(jnp.arange(flat_count))
    lower = (flat_axis[:, None] > flat_axis[None, :]).astype(jnp.bfloat16)
    before = jnp.einsum(
        "ij,bjs->bis", lower, selected.astype(jnp.bfloat16), preferred_element_type=jnp.float32
    )
    position = (
        jnp.sum(jnp.where(selected, before, jnp.float32(0.0)), axis=-1)
        .astype(jnp.int32)
        .reshape(blocks, row_count, topk_all)
    )
    capacity = (
        jnp.sum(jnp.where(target_slot[..., None] == slot_axis, cap_blocks, 0), axis=-1) * cap_unit
    )
    retained = position < capacity
    return (gates, target_slot, position, retained)


def unit_plan(slot_local, n_dp, hidden_units):
    chunks = n_dp // math.gcd(slot_local, n_dp)
    units_per = slot_local * chunks // n_dp
    chunk_width = hidden_units // chunks
    owned = [[((o * units_per + i) // chunks, (o * units_per + i) % chunks) for i in range(units_per)]
             for o in range(n_dp)]
    first_slot = [owned[o][0][0] for o in range(n_dp)]
    slots_per = max(owned[o][-1][0] - first_slot[o] + 1 for o in range(n_dp))
    return chunks, units_per, chunk_width, owned, first_slot, slots_per


def on_device(
    context,
    w_proj,
    residual,
    gain_first,
    gain_next,
    w_router,
    expert_ids,
    replica_pick,
    slot_expert,
    cap_blocks,
    w_in,
    w_out,
):
    tok_rows, model_width = residual.shape
    topk_all = expert_ids.shape[1]
    slot_local, d_local, _ = w_in.shape
    hidden_units = w_in.shape[2] // 2
    ff_local = w_out.shape[1]
    n_dp = lax.axis_size("dp")
    n_exp = lax.axis_size("expert")
    dp_at = lax.axis_index("dp")
    exp_at = lax.axis_index("expert")
    chunks, units_per, chunk_width, owned, first_slot, slots_per = unit_plan(
        slot_local, n_dp, hidden_units
    )
    sources_per_chunk = chunk_width // ff_local

    win_parts, wout_parts = [], []
    for o in range(n_dp):
        win_units, wout_units = [], []
        for s, c in owned[o]:
            lo = c * chunk_width
            win_units.append(
                jnp.concatenate(
                    [w_in[s, :, lo:lo + chunk_width],
                     w_in[s, :, hidden_units + lo:hidden_units + lo + chunk_width]],
                    axis=-1,
                )
            )
            wout_units.append(w_out[s])
        win_parts.append(jnp.stack(win_units))
        wout_parts.append(jnp.stack(wout_units))
    win_send = jnp.stack(win_parts)
    wout_send = jnp.stack(wout_parts)
    both_recv = lax.all_to_all(
        jnp.stack([win_send, wout_send.reshape(win_send.shape)], axis=2), "dp", 0, 0, tiled=True
    )
    win_recv = both_recv[:, :, 0]
    wout_recv = both_recv[:, :, 1].reshape(wout_send.shape)
    unit_in = win_recv.transpose(1, 0, 2, 3).reshape(units_per, n_dp * d_local, 2 * chunk_width)

    ids_all = lax.all_gather(
        jnp.concatenate([expert_ids, replica_pick], axis=1), "expert", axis=0, tiled=True
    ).reshape(n_exp, tok_rows, 2 * topk_all)

    flat_context = context.reshape(-1, context.shape[3])
    attended = lax.psum_scatter(
        jnp.dot(flat_context, w_proj, preferred_element_type=jnp.float32).astype(jnp.bfloat16),
        "dp",
        scatter_dimension=0,
        tiled=True,
    )
    hidden_state = (residual.astype(jnp.float32) + attended.astype(jnp.float32)).astype(
        jnp.bfloat16
    )
    normed = rms_scale(hidden_state, gain_first).astype(jnp.bfloat16)

    normed_all = lax.all_gather(normed, "expert", axis=0, tiled=True)
    gates, target_slot, position, retained = route_rows(
        normed_all,
        w_router,
        ids_all[:, :, :topk_all],
        ids_all[:, :, topk_all:],
        slot_expert,
        cap_blocks,
        CAP_UNIT,
    )
    here = retained & (target_slot // slot_local == exp_at)
    local = jnp.where(here, (target_slot % slot_local) * CAP_MOST + position, -1)
    hit = local[..., None] == jnp.arange(slot_local * CAP_MOST)
    pick = jnp.any(hit, axis=2).astype(jnp.bfloat16)
    weight = jnp.sum(jnp.where(hit, gates[..., None], jnp.float32(0.0)), axis=2)
    slot_in = jnp.einsum(
        "btr,btd->brd",
        pick,
        normed_all.reshape(n_exp, tok_rows, model_width),
        preferred_element_type=jnp.float32,
    ).astype(jnp.bfloat16)
    slot_in = slot_in.reshape(n_exp, slot_local, CAP_MOST, model_width)

    x_parts = []
    for o in range(n_dp):
        x_parts.append(
            jnp.stack(
                [slot_in[:, min(first_slot[o] + j, slot_local - 1)] for j in range(slots_per)]
            )
        )
    x_recv = lax.all_to_all(jnp.stack(x_parts), "dp", 0, 0, tiled=True)

    unit_rows = n_dp * n_exp * CAP_MOST
    y_acc = jnp.zeros((slots_per, unit_rows, model_width), jnp.float32)
    my_first = (dp_at * units_per) // chunks
    for i in range(units_per):
        unit = dp_at * units_per + i
        slot_at = unit // chunks - my_first
        chunk_at = unit % chunks
        rows = lax.dynamic_index_in_dim(x_recv, slot_at, axis=1, keepdims=False)
        rows = rows.reshape(unit_rows, model_width)
        w_down = lax.dynamic_slice_in_dim(
            wout_recv[:, i], chunk_at * sources_per_chunk, sources_per_chunk, axis=0
        ).reshape(chunk_width, model_width)
        gate_up = jnp.dot(rows, unit_in[i], preferred_element_type=jnp.float32)
        activated = (
            jax.nn.silu(gate_up[:, :chunk_width]) * gate_up[:, chunk_width:]
        ).astype(jnp.bfloat16)
        out = jnp.dot(activated, w_down, preferred_element_type=jnp.float32)
        prev = lax.dynamic_index_in_dim(y_acc, slot_at, axis=0, keepdims=False)
        y_acc = lax.dynamic_update_index_in_dim(y_acc, prev + out, slot_at, axis=0)

    y_send = (
        y_acc.reshape(slots_per, n_dp, n_exp, CAP_MOST, model_width)
        .transpose(1, 0, 2, 3, 4)
        .astype(jnp.bfloat16)
    )
    y_recv = lax.all_to_all(y_send, "dp", 0, 0, tiled=True)
    slot_out = [None] * slot_local
    for o in range(n_dp):
        mine = {s for s, _ in owned[o]}
        for j in range(slots_per):
            s = first_slot[o] + j
            if s < slot_local and s in mine:
                part = y_recv[o, j].astype(jnp.float32)
                slot_out[s] = part if slot_out[s] is None else slot_out[s] + part
    expert_out = (
        jnp.stack(slot_out, axis=1)
        .reshape(n_exp, slot_local * CAP_MOST, model_width)
        .astype(jnp.bfloat16)
    )

    weight_hi = weight.astype(jnp.bfloat16)
    weight_lo = (weight - weight_hi.astype(jnp.float32)).astype(jnp.bfloat16)
    partial = jnp.einsum(
        "btr,brd->btd", weight_hi, expert_out, preferred_element_type=jnp.float32
    ) + jnp.einsum("btr,brd->btd", weight_lo, expert_out, preferred_element_type=jnp.float32)
    combined = lax.psum_scatter(
        partial.reshape(n_exp * tok_rows, model_width).astype(jnp.bfloat16),
        "expert",
        scatter_dimension=0,
        tiled=True,
    )
    residual_out = (hidden_state.astype(jnp.float32) + combined.astype(jnp.float32)).astype(
        jnp.bfloat16
    )
    next_normed = rms_scale(residual_out, gain_next).astype(jnp.bfloat16)
    return (residual_out, next_normed)


def solution(mesh):
    placed = (
        P("expert", None, None, "dp"),
        P("dp", None),
        P(("dp", "expert"), None),
        P(),
        P(),
        P(),
        P(("dp", "expert"), None),
        P(("dp", "expert"), None),
        P(),
        P(),
        P("expert", "dp", None),
        P("expert", "dp", None),
    )
    return jax.shard_map(
        on_device,
        mesh=mesh,
        in_specs=placed,
        out_specs=(P(("dp", "expert"), None), P(("dp", "expert"), None)),
        check_vma=False,
    )
```

```python
import math

import jax
import jax.numpy as jnp
from jax import lax
from jax.sharding import PartitionSpec as P

CAP_UNIT = 8
CAP_MOST = 32


def rms_scale(values, gain):
    widened = values.astype(jnp.float32)
    return widened * lax.rsqrt(jnp.mean(widened * widened, axis=-1, keepdims=True) + 1e-06) * gain


def route_rows(normed, w_router, expert_ids, replica_pick, slot_expert, cap_blocks, cap_unit):
    blocks, row_count, topk_all = expert_ids.shape
    experts_all = w_router.shape[1]
    slots_all = slot_expert.shape[0]
    logits = jnp.dot(normed, w_router, preferred_element_type=jnp.float32)
    logits = logits.reshape(blocks, row_count, experts_all)
    expert_axis = jnp.arange(experts_all)
    one_hot = expert_ids[..., None] == expert_axis
    chosen = jnp.sum(jnp.where(one_hot, logits[:, :, None, :], jnp.float32(0.0)), axis=-1)
    raised = jnp.exp(chosen)
    gates = raised / jnp.sum(raised, axis=-1, keepdims=True)
    holder = (slot_expert[None, :] == expert_axis[:, None]).astype(jnp.int32)
    rep_count = jnp.sum(holder, axis=1)
    earlier = jnp.cumsum(holder, axis=1) - holder
    slot_rank = jnp.sum(earlier * holder, axis=0)
    count_of = jnp.sum(jnp.where(one_hot, rep_count, 0), axis=-1)
    replica = replica_pick % count_of
    slot_axis = jnp.arange(slots_all)
    matched = (slot_expert == expert_ids[..., None]) & (slot_rank == replica[..., None])
    target_slot = jnp.sum(jnp.where(matched, slot_axis, 0), axis=-1)
    flat_count = row_count * topk_all
    selected = matched.reshape(blocks, flat_count, slots_all)
    flat_axis = lax.optimization_barrier(jnp.arange(flat_count))
    lower = (flat_axis[:, None] > flat_axis[None, :]).astype(jnp.bfloat16)
    before = jnp.einsum(
        "ij,bjs->bis", lower, selected.astype(jnp.bfloat16), preferred_element_type=jnp.float32
    )
    position = (
        jnp.sum(jnp.where(selected, before, jnp.float32(0.0)), axis=-1)
        .astype(jnp.int32)
        .reshape(blocks, row_count, topk_all)
    )
    capacity = (
        jnp.sum(jnp.where(target_slot[..., None] == slot_axis, cap_blocks, 0), axis=-1) * cap_unit
    )
    retained = position < capacity
    return (gates, target_slot, position, retained)


def unit_plan(slot_local, n_dp, hidden_units):
    full = slot_local // n_dp
    rest = slot_local - full * n_dp
    chunks = n_dp // math.gcd(rest, n_dp) if rest else 1
    halves = rest * chunks // n_dp
    chunk_width = hidden_units // chunks
    owned_full = [[o * full + j for j in range(full)] for o in range(n_dp)]
    owned_part = [
        [(full * n_dp + (o * halves + i) // chunks, (o * halves + i) % chunks) for i in range(halves)]
        for o in range(n_dp)
    ]
    return full, halves, chunks, chunk_width, owned_full, owned_part


def on_device(
    context,
    w_proj,
    residual,
    gain_first,
    gain_next,
    w_router,
    expert_ids,
    replica_pick,
    slot_expert,
    cap_blocks,
    w_in,
    w_out,
):
    tok_rows, model_width = residual.shape
    topk_all = expert_ids.shape[1]
    slot_local, d_local, _ = w_in.shape
    hidden_units = w_in.shape[2] // 2
    ff_local = w_out.shape[1]
    n_dp = lax.axis_size("dp")
    n_exp = lax.axis_size("expert")
    dp_at = lax.axis_index("dp")
    exp_at = lax.axis_index("expert")
    full, halves, chunks, chunk_width, owned_full, owned_part = unit_plan(
        slot_local, n_dp, hidden_units
    )
    sources_per_chunk = chunk_width // ff_local
    lane_width = 2 * chunk_width if (ff_local * model_width) % (2 * chunk_width) == 0 else 128

    def as_rows(piece):
        return piece.reshape(-1, lane_width)

    weight_parts = []
    for o in range(n_dp):
        pieces = []
        for s in owned_full[o]:
            pieces += [as_rows(w_in[s]), as_rows(w_out[s])]
        for s, c in owned_part[o]:
            lo = c * chunk_width
            pieces += [
                as_rows(w_in[s, :, lo:lo + chunk_width]),
                as_rows(w_in[s, :, hidden_units + lo:hidden_units + lo + chunk_width]),
                as_rows(w_out[s]),
            ]
        weight_parts.append(jnp.concatenate(pieces, axis=0))
    weight_recv = lax.all_to_all(jnp.stack(weight_parts), "dp", 0, 0, tiled=True)
    offset = 0

    def take(shape):
        nonlocal offset
        count = math.prod(shape) // lane_width
        piece = weight_recv[:, offset:offset + count].reshape((n_dp,) + shape)
        offset += count
        return piece

    full_in, full_out, part_in, part_out = [], [], [], []
    for _ in range(full):
        full_in.append(take((d_local, 2 * hidden_units)).reshape(n_dp * d_local, 2 * hidden_units))
        full_out.append(take((ff_local, model_width)).reshape(n_dp * ff_local, model_width))
    for _ in range(halves):
        gate_in = take((d_local, chunk_width))
        up_in = take((d_local, chunk_width))
        part_in.append(
            jnp.concatenate([gate_in, up_in], axis=-1).reshape(n_dp * d_local, 2 * chunk_width)
        )
        part_out.append(take((ff_local, model_width)))

    ids_all = lax.all_gather(
        jnp.concatenate([expert_ids, replica_pick], axis=1), "expert", axis=0, tiled=True
    ).reshape(n_exp, tok_rows, 2 * topk_all)

    flat_context = context.reshape(-1, context.shape[3])
    attended = lax.psum_scatter(
        jnp.dot(flat_context, w_proj, preferred_element_type=jnp.float32).astype(jnp.bfloat16),
        "dp",
        scatter_dimension=0,
        tiled=True,
    )
    hidden_state = (residual.astype(jnp.float32) + attended.astype(jnp.float32)).astype(
        jnp.bfloat16
    )
    normed = rms_scale(hidden_state, gain_first).astype(jnp.bfloat16)

    normed_all = lax.all_gather(normed, "expert", axis=0, tiled=True)
    gates, target_slot, position, retained = route_rows(
        normed_all,
        w_router,
        ids_all[:, :, :topk_all],
        ids_all[:, :, topk_all:],
        slot_expert,
        cap_blocks,
        CAP_UNIT,
    )
    here = retained & (target_slot // slot_local == exp_at)
    local = jnp.where(here, (target_slot % slot_local) * CAP_MOST + position, -1)
    hit = local[..., None] == jnp.arange(slot_local * CAP_MOST)
    pick = jnp.any(hit, axis=2).astype(jnp.bfloat16)
    weight = jnp.sum(jnp.where(hit, gates[..., None], jnp.float32(0.0)), axis=2)
    slot_in = jnp.einsum(
        "btr,btd->brd",
        pick,
        normed_all.reshape(n_exp, tok_rows, model_width),
        preferred_element_type=jnp.float32,
    ).astype(jnp.bfloat16)
    slot_in = slot_in.reshape(n_exp, slot_local, CAP_MOST, model_width)

    x_parts = []
    for o in range(n_dp):
        x_parts.append(
            jnp.stack([slot_in[:, s] for s in owned_full[o]] + [slot_in[:, s] for s, _ in owned_part[o]])
        )
    x_recv = lax.all_to_all(jnp.stack(x_parts), "dp", 0, 0, tiled=True)

    unit_rows = n_dp * n_exp * CAP_MOST

    def expert_rows(rows, w_up, w_down, width):
        gate_up = jnp.dot(rows, w_up, preferred_element_type=jnp.float32)
        activated = (jax.nn.silu(gate_up[:, :width]) * gate_up[:, width:]).astype(jnp.bfloat16)
        return jnp.dot(activated, w_down, preferred_element_type=jnp.float32).astype(jnp.bfloat16)

    outs = []
    for j in range(full):
        rows = x_recv[:, j].reshape(unit_rows, model_width)
        outs.append(expert_rows(rows, full_in[j], full_out[j], hidden_units))
    for i in range(halves):
        rows = x_recv[:, full + i].reshape(unit_rows, model_width)
        chunk_at = (dp_at * halves + i) % chunks
        w_down = lax.dynamic_slice_in_dim(
            part_out[i], chunk_at * sources_per_chunk, sources_per_chunk, axis=0
        ).reshape(chunk_width, model_width)
        outs.append(expert_rows(rows, part_in[i], w_down, chunk_width))
    y_send = (
        jnp.stack(outs)
        .reshape(full + halves, n_dp, n_exp, CAP_MOST, model_width)
        .transpose(1, 0, 2, 3, 4)
    )
    y_recv = lax.all_to_all(y_send, "dp", 0, 0, tiled=True)
    slot_out = [None] * slot_local
    for o in range(n_dp):
        for j, s in enumerate(owned_full[o]):
            slot_out[s] = y_recv[o, j]
        for i, (s, _) in enumerate(owned_part[o]):
            part = y_recv[o, full + i].astype(jnp.float32)
            slot_out[s] = part if slot_out[s] is None else slot_out[s] + part
    slot_out = [part.astype(jnp.bfloat16) for part in slot_out]
    expert_out = (
        jnp.stack(slot_out, axis=1)
        .reshape(n_exp, slot_local * CAP_MOST, model_width)
        .astype(jnp.bfloat16)
    )

    weight_hi = weight.astype(jnp.bfloat16)
    weight_lo = (weight - weight_hi.astype(jnp.float32)).astype(jnp.bfloat16)
    partial = jnp.einsum(
        "btr,brd->btd", weight_hi, expert_out, preferred_element_type=jnp.float32
    ) + jnp.einsum("btr,brd->btd", weight_lo, expert_out, preferred_element_type=jnp.float32)
    combined = lax.psum_scatter(
        partial.reshape(n_exp * tok_rows, model_width),
        "expert",
        scatter_dimension=0,
        tiled=True,
    )
    residual_out = (hidden_state.astype(jnp.float32) + combined.astype(jnp.float32)).astype(
        jnp.bfloat16
    )
    next_normed = rms_scale(residual_out, gain_next).astype(jnp.bfloat16)
    return (residual_out, next_normed)


def solution(mesh):
    placed = (
        P("expert", None, None, "dp"),
        P("dp", None),
        P(("dp", "expert"), None),
        P(),
        P(),
        P(),
        P(("dp", "expert"), None),
        P(("dp", "expert"), None),
        P(),
        P(),
        P("expert", "dp", None),
        P("expert", "dp", None),
    )
    return jax.shard_map(
        on_device,
        mesh=mesh,
        in_specs=placed,
        out_specs=(P(("dp", "expert"), None), P(("dp", "expert"), None)),
        check_vma=False,
    )
```

```python
import math

import jax
import jax.numpy as jnp
from jax import lax
from jax.sharding import PartitionSpec as P


CAP_UNIT = 8
CAP_MOST = 32


def rms_scale(values, gain):
    widened = values.astype(jnp.float32)
    return widened * lax.rsqrt(jnp.mean(widened * widened, axis=-1, keepdims=True) + 1e-06) * gain


def route_rows(normed, w_router, expert_ids, replica_pick, slot_expert, cap_blocks, cap_unit):
    blocks, row_count, topk_all = expert_ids.shape
    experts_all = w_router.shape[1]
    slots_all = slot_expert.shape[0]
    logits = jnp.dot(normed, w_router, preferred_element_type=jnp.float32)
    logits = logits.reshape(blocks, row_count, experts_all)
    expert_axis = jnp.arange(experts_all)
    one_hot = expert_ids[..., None] == expert_axis
    chosen = jnp.sum(jnp.where(one_hot, logits[:, :, None, :], jnp.float32(0.0)), axis=-1)
    raised = jnp.exp(chosen)
    gates = raised / jnp.sum(raised, axis=-1, keepdims=True)
    holder = (slot_expert[None, :] == expert_axis[:, None]).astype(jnp.int32)
    rep_count = jnp.sum(holder, axis=1)
    earlier = jnp.cumsum(holder, axis=1) - holder
    slot_rank = jnp.sum(earlier * holder, axis=0)
    count_of = jnp.sum(jnp.where(one_hot, rep_count, 0), axis=-1)
    replica = replica_pick % count_of
    slot_axis = jnp.arange(slots_all)
    matched = (slot_expert == expert_ids[..., None]) & (slot_rank == replica[..., None])
    target_slot = jnp.sum(jnp.where(matched, slot_axis, 0), axis=-1)
    flat_count = row_count * topk_all
    selected = matched.reshape(blocks, flat_count, slots_all)
    flat_axis = lax.optimization_barrier(jnp.arange(flat_count))
    lower = (flat_axis[:, None] > flat_axis[None, :]).astype(jnp.bfloat16)
    before = jnp.einsum(
        "ij,bjs->bis", lower, selected.astype(jnp.bfloat16), preferred_element_type=jnp.float32
    )
    position = (
        jnp.sum(jnp.where(selected, before, jnp.float32(0.0)), axis=-1)
        .astype(jnp.int32)
        .reshape(blocks, row_count, topk_all)
    )
    capacity = (
        jnp.sum(jnp.where(target_slot[..., None] == slot_axis, cap_blocks, 0), axis=-1) * cap_unit
    )
    retained = position < capacity
    return (gates, target_slot, position, retained)


def unit_plan(slot_local, n_dp, hidden_units):
    full = slot_local // n_dp
    rest = slot_local - full * n_dp
    chunks = n_dp // math.gcd(rest, n_dp) if rest else 1
    halves = rest * chunks // n_dp
    chunk_width = hidden_units // chunks
    owned_full = [[o * full + j for j in range(full)] for o in range(n_dp)]
    owned_part = [
        [(full * n_dp + (o * halves + i) // chunks, (o * halves + i) % chunks) for i in range(halves)]
        for o in range(n_dp)
    ]
    return full, halves, chunks, chunk_width, owned_full, owned_part


def on_device_body(
    context,
    w_proj,
    residual,
    gain_first,
    gain_next,
    w_router,
    expert_ids,
    replica_pick,
    slot_expert,
    cap_blocks,
    w_in,
    w_out,
):
    tok_rows, model_width = residual.shape
    topk_all = expert_ids.shape[1]
    slot_local, d_local, _ = w_in.shape
    hidden_units = w_in.shape[2] // 2
    ff_local = w_out.shape[1]
    n_dp = lax.axis_size("dp")
    n_exp = lax.axis_size("expert")
    dp_at = lax.axis_index("dp")
    exp_at = lax.axis_index("expert")
    full, halves, chunks, chunk_width, owned_full, owned_part = unit_plan(
        slot_local, n_dp, hidden_units
    )
    sources_per_chunk = chunk_width // ff_local
    lane_width = 2 * chunk_width if (ff_local * model_width) % (2 * chunk_width) == 0 else 128

    def as_rows(piece):
        return piece.reshape(-1, lane_width)

    weight_parts = []
    for o in range(n_dp):
        pieces = []
        for s in owned_full[o]:
            pieces += [as_rows(w_in[s]), as_rows(w_out[s])]
        for s, c in owned_part[o]:
            lo = c * chunk_width
            pieces += [
                as_rows(w_in[s, :, lo:lo + chunk_width]),
                as_rows(w_in[s, :, hidden_units + lo:hidden_units + lo + chunk_width]),
                as_rows(w_out[s]),
            ]
        weight_parts.append(jnp.concatenate(pieces, axis=0))
    weight_recv = lax.all_to_all(jnp.stack(weight_parts), "dp", 0, 0, tiled=True)
    offset = 0

    def take(shape):
        nonlocal offset
        count = math.prod(shape) // lane_width
        piece = weight_recv[:, offset:offset + count].reshape((n_dp,) + shape)
        offset += count
        return piece

    full_in, full_out, part_in, part_out = [], [], [], []
    for _ in range(full):
        full_in.append(take((d_local, 2 * hidden_units)).reshape(n_dp * d_local, 2 * hidden_units))
        full_out.append(take((ff_local, model_width)).reshape(n_dp * ff_local, model_width))
    for _ in range(halves):
        gate_in = take((d_local, chunk_width))
        up_in = take((d_local, chunk_width))
        part_in.append(
            jnp.concatenate([gate_in, up_in], axis=-1).reshape(n_dp * d_local, 2 * chunk_width)
        )
        part_out.append(take((ff_local, model_width)))

    ids_all = lax.all_gather(
        jnp.concatenate([expert_ids, replica_pick], axis=1), "expert", axis=0, tiled=True
    ).reshape(n_exp, tok_rows, 2 * topk_all)

    flat_context = context.reshape(-1, context.shape[3])
    attended = lax.psum_scatter(
        jnp.dot(flat_context, w_proj, preferred_element_type=jnp.float32),
        "dp",
        scatter_dimension=0,
        tiled=True,
    )
    hidden_state = (residual.astype(jnp.float32) + attended.astype(jnp.float32)).astype(
        jnp.bfloat16
    )
    normed = rms_scale(hidden_state, gain_first).astype(jnp.bfloat16)

    normed_all = lax.all_gather(normed, "expert", axis=0, tiled=True)
    gates, target_slot, position, retained = route_rows(
        normed_all,
        w_router,
        ids_all[:, :, :topk_all],
        ids_all[:, :, topk_all:],
        slot_expert,
        cap_blocks,
        CAP_UNIT,
    )
    here = retained & (target_slot // slot_local == exp_at)
    local = jnp.where(here, (target_slot % slot_local) * CAP_MOST + position, -1)
    hit = local[..., None] == jnp.arange(slot_local * CAP_MOST)
    pick = jnp.any(hit, axis=2).astype(jnp.bfloat16)
    weight = jnp.sum(jnp.where(hit, gates[..., None], jnp.float32(0.0)), axis=2)
    slot_in = jnp.einsum(
        "btr,btd->brd",
        pick,
        normed_all.reshape(n_exp, tok_rows, model_width),
        preferred_element_type=jnp.float32,
    ).astype(jnp.bfloat16)
    slot_in = slot_in.reshape(n_exp, slot_local, CAP_MOST, model_width)

    x_parts = []
    for o in range(n_dp):
        x_parts.append(
            jnp.stack([slot_in[:, s] for s in owned_full[o]] + [slot_in[:, s] for s, _ in owned_part[o]])
        )
    x_recv = lax.all_to_all(jnp.stack(x_parts), "dp", 0, 0, tiled=True)

    unit_rows = n_dp * n_exp * CAP_MOST

    def expert_rows(rows, w_up, w_down, width):
        gate_up = jnp.dot(rows, w_up, preferred_element_type=jnp.float32)
        activated = (jax.nn.silu(gate_up[:, :width]) * gate_up[:, width:]).astype(jnp.bfloat16)
        return jnp.dot(activated, w_down, preferred_element_type=jnp.float32).astype(jnp.bfloat16)

    outs = []
    for j in range(full):
        rows = x_recv[:, j].reshape(unit_rows, model_width)
        outs.append(expert_rows(rows, full_in[j], full_out[j], hidden_units))
    for i in range(halves):
        rows = x_recv[:, full + i].reshape(unit_rows, model_width)
        chunk_at = (dp_at * halves + i) % chunks
        w_down = lax.dynamic_slice_in_dim(
            part_out[i], chunk_at * sources_per_chunk, sources_per_chunk, axis=0
        ).reshape(chunk_width, model_width)
        outs.append(expert_rows(rows, part_in[i], w_down, chunk_width))
    y_send = (
        jnp.stack(outs)
        .reshape(full + halves, n_dp, n_exp, CAP_MOST, model_width)
        .transpose(1, 0, 2, 3, 4)
    )
    weight_hi = weight.astype(jnp.bfloat16)
    weight_lo = (weight - weight_hi.astype(jnp.float32)).astype(jnp.bfloat16)
    halves_d = 4 if model_width % 512 == 0 else 1
    piece_width = model_width // halves_d
    combined_parts = []
    for h in range(halves_d):
        cols = slice(h * piece_width, (h + 1) * piece_width)
        y_recv = lax.all_to_all(y_send[..., cols], "dp", 0, 0, tiled=True)
        slot_out = [None] * slot_local
        for o in range(n_dp):
            for j, s in enumerate(owned_full[o]):
                slot_out[s] = y_recv[o, j]
            for i, (s, _) in enumerate(owned_part[o]):
                part = y_recv[o, full + i].astype(jnp.float32)
                slot_out[s] = part if slot_out[s] is None else slot_out[s] + part
        slot_out = [part.astype(jnp.bfloat16) for part in slot_out]
        expert_out = jnp.stack(slot_out, axis=1).reshape(
            n_exp, slot_local * CAP_MOST, piece_width
        )
        partial = jnp.einsum(
            "btr,brd->btd", weight_hi, expert_out, preferred_element_type=jnp.float32
        ) + jnp.einsum("btr,brd->btd", weight_lo, expert_out, preferred_element_type=jnp.float32)
        combined_parts.append(
            lax.psum_scatter(
                partial.reshape(n_exp * tok_rows, piece_width).astype(jnp.bfloat16),
                "expert",
                scatter_dimension=0,
                tiled=True,
            )
        )
    combined = jnp.concatenate(combined_parts, axis=-1)
    residual_out = (hidden_state.astype(jnp.float32) + combined.astype(jnp.float32)).astype(
        jnp.bfloat16
    )
    next_normed = rms_scale(residual_out, gain_next).astype(jnp.bfloat16)
    return (residual_out, next_normed)


def solution(mesh):
    placed = (
        P("expert", None, None, "dp"),
        P("dp", None),
        P(("dp", "expert"), None),
        P(),
        P(),
        P(),
        P(("dp", "expert"), None),
        P(("dp", "expert"), None),
        P(),
        P(),
        P("expert", "dp", None),
        P("expert", "dp", None),
    )
    return jax.shard_map(
        on_device_body,
        mesh=mesh,
        in_specs=placed,
        out_specs=(P(("dp", "expert"), None), P(("dp", "expert"), None)),
        check_vma=False,
    )
```

```python
import math

import jax
import jax.numpy as jnp
from jax import lax
from jax.sharding import PartitionSpec as P


CAP_UNIT = 8
CAP_MOST = 32


def rms_scale(values, gain):
    widened = values.astype(jnp.float32)
    return widened * lax.rsqrt(jnp.mean(widened * widened, axis=-1, keepdims=True) + 1e-06) * gain


def route_rows(normed, w_router, expert_ids, replica_pick, slot_expert, cap_blocks, cap_unit):
    blocks, row_count, topk_all = expert_ids.shape
    experts_all = w_router.shape[1]
    slots_all = slot_expert.shape[0]
    logits = jnp.dot(normed, w_router, preferred_element_type=jnp.float32)
    logits = logits.reshape(blocks, row_count, experts_all)
    expert_axis = jnp.arange(experts_all)
    one_hot = expert_ids[..., None] == expert_axis
    chosen = jnp.sum(jnp.where(one_hot, logits[:, :, None, :], jnp.float32(0.0)), axis=-1)
    raised = jnp.exp(chosen)
    gates = raised / jnp.sum(raised, axis=-1, keepdims=True)
    holder = (slot_expert[None, :] == expert_axis[:, None]).astype(jnp.int32)
    rep_count = jnp.sum(holder, axis=1)
    earlier = jnp.cumsum(holder, axis=1) - holder
    slot_rank = jnp.sum(earlier * holder, axis=0)
    count_of = jnp.sum(jnp.where(one_hot, rep_count, 0), axis=-1)
    replica = replica_pick % count_of
    slot_axis = jnp.arange(slots_all)
    matched = (slot_expert == expert_ids[..., None]) & (slot_rank == replica[..., None])
    target_slot = jnp.sum(jnp.where(matched, slot_axis, 0), axis=-1)
    flat_count = row_count * topk_all
    selected = matched.reshape(blocks, flat_count, slots_all)
    flat_axis = lax.optimization_barrier(jnp.arange(flat_count))
    lower = (flat_axis[:, None] > flat_axis[None, :]).astype(jnp.bfloat16)
    before = jnp.einsum(
        "ij,bjs->bis", lower, selected.astype(jnp.bfloat16), preferred_element_type=jnp.float32
    )
    position = (
        jnp.sum(jnp.where(selected, before, jnp.float32(0.0)), axis=-1)
        .astype(jnp.int32)
        .reshape(blocks, row_count, topk_all)
    )
    capacity = (
        jnp.sum(jnp.where(target_slot[..., None] == slot_axis, cap_blocks, 0), axis=-1) * cap_unit
    )
    retained = position < capacity
    return (gates, target_slot, position, retained)


def unit_plan(slot_local, n_dp, hidden_units):
    full = slot_local // n_dp
    rest = slot_local - full * n_dp
    chunks = n_dp // math.gcd(rest, n_dp) if rest else 1
    halves = rest * chunks // n_dp
    chunk_width = hidden_units // chunks
    owned_full = [[o * full + j for j in range(full)] for o in range(n_dp)]
    if halves == 1 and rest * chunks == n_dp:
        owned_part = [[(full * n_dp + o % rest, o // rest)] for o in range(n_dp)]
    else:
        owned_part = [
            [(full * n_dp + (o * halves + i) // chunks, (o * halves + i) % chunks)
             for i in range(halves)]
            for o in range(n_dp)
        ]
    return full, halves, chunks, chunk_width, owned_full, owned_part


def on_device_body(
    context,
    w_proj,
    residual,
    gain_first,
    gain_next,
    w_router,
    expert_ids,
    replica_pick,
    slot_expert,
    cap_blocks,
    w_in,
    w_out,
):
    tok_rows, model_width = residual.shape
    topk_all = expert_ids.shape[1]
    slot_local, d_local, _ = w_in.shape
    hidden_units = w_in.shape[2] // 2
    ff_local = w_out.shape[1]
    n_dp = lax.axis_size("dp")
    n_exp = lax.axis_size("expert")
    dp_at = lax.axis_index("dp")
    exp_at = lax.axis_index("expert")
    full, halves, chunks, chunk_width, owned_full, owned_part = unit_plan(
        slot_local, n_dp, hidden_units
    )
    sources_per_chunk = chunk_width // ff_local
    rest = slot_local - full * n_dp
    paired = (
        halves == 1 and rest * chunks == n_dp and chunk_width == rest * ff_local
    )
    lane_width = 2 * chunk_width if (ff_local * model_width) % (2 * chunk_width) == 0 else 128

    def as_rows(piece):
        return piece.reshape(-1, lane_width)

    weight_parts = []
    for o in range(n_dp):
        pieces = []
        for s in owned_full[o]:
            pieces += [as_rows(w_in[s]), as_rows(w_out[s])]
        for s, c in owned_part[o]:
            lo = c * chunk_width
            pieces += [
                as_rows(w_in[s, :, lo:lo + chunk_width]),
                as_rows(w_in[s, :, hidden_units + lo:hidden_units + lo + chunk_width]),
            ]
            if not paired:
                pieces.append(as_rows(w_out[s]))
        weight_parts.append(jnp.concatenate(pieces, axis=0))
    weight_recv = lax.all_to_all(jnp.stack(weight_parts), "dp", 0, 0, tiled=True)
    offset = 0

    def take(shape):
        nonlocal offset
        count = math.prod(shape) // lane_width
        piece = weight_recv[:, offset:offset + count].reshape((n_dp,) + shape)
        offset += count
        return piece

    full_in, full_out, part_in, part_out = [], [], [], []
    for _ in range(full):
        full_in.append(take((d_local, 2 * hidden_units)).reshape(n_dp * d_local, 2 * hidden_units))
        full_out.append(take((ff_local, model_width)).reshape(n_dp * ff_local, model_width))
    for _ in range(halves):
        gate_in = take((d_local, chunk_width))
        up_in = take((d_local, chunk_width))
        part_in.append(
            jnp.concatenate([gate_in, up_in], axis=-1).reshape(n_dp * d_local, 2 * chunk_width)
        )
        if not paired:
            part_out.append(take((ff_local, model_width)))
    if paired:
        group_at = dp_at % rest
        held = [lax.dynamic_index_in_dim(w_out, full * n_dp + group_at, 0, keepdims=False)]
        for k in range(1, rest):
            sent = lax.dynamic_index_in_dim(
                w_out, full * n_dp + (group_at + rest - k) % rest, 0, keepdims=False
            )
            pairs = [
                (base + (p + k) % rest, base + p)
                for base in range(0, n_dp, rest)
                for p in range(rest)
            ]
            held.append(lax.ppermute(sent, "dp", pairs))
        part_out.append(
            jnp.roll(jnp.stack(held), group_at, axis=0).reshape(chunk_width, model_width)
        )

    ids_all = lax.all_gather(
        jnp.concatenate([expert_ids, replica_pick], axis=1), "expert", axis=0, tiled=True
    ).reshape(n_exp, tok_rows, 2 * topk_all)

    flat_context = context.reshape(-1, context.shape[3])
    attended = lax.psum_scatter(
        jnp.dot(flat_context, w_proj, preferred_element_type=jnp.float32),
        "dp",
        scatter_dimension=0,
        tiled=True,
    )
    hidden_state = (residual.astype(jnp.float32) + attended.astype(jnp.float32)).astype(
        jnp.bfloat16
    )
    normed = rms_scale(hidden_state, gain_first).astype(jnp.bfloat16)

    normed_all = lax.all_gather(normed, "expert", axis=0, tiled=True)
    gates, target_slot, position, retained = route_rows(
        normed_all,
        w_router,
        ids_all[:, :, :topk_all],
        ids_all[:, :, topk_all:],
        slot_expert,
        cap_blocks,
        CAP_UNIT,
    )
    here = retained & (target_slot // slot_local == exp_at)
    local = jnp.where(here, (target_slot % slot_local) * CAP_MOST + position, -1)
    hit = local[..., None] == jnp.arange(slot_local * CAP_MOST)
    pick = jnp.any(hit, axis=2).astype(jnp.bfloat16)
    weight = jnp.sum(jnp.where(hit, gates[..., None], jnp.float32(0.0)), axis=2)
    slot_in = jnp.einsum(
        "btr,btd->brd",
        pick,
        normed_all.reshape(n_exp, tok_rows, model_width),
        preferred_element_type=jnp.float32,
    ).astype(jnp.bfloat16)
    slot_in = slot_in.reshape(n_exp, slot_local, CAP_MOST, model_width)

    x_parts = []
    for o in range(n_dp):
        x_parts.append(
            jnp.stack([slot_in[:, s] for s in owned_full[o]] + [slot_in[:, s] for s, _ in owned_part[o]])
        )
    x_recv = lax.all_to_all(jnp.stack(x_parts), "dp", 0, 0, tiled=True)

    unit_rows = n_dp * n_exp * CAP_MOST

    def expert_rows(rows, w_up, w_down, width):
        gate_up = jnp.dot(rows, w_up, preferred_element_type=jnp.float32)
        activated = (jax.nn.silu(gate_up[:, :width]) * gate_up[:, width:]).astype(jnp.bfloat16)
        return jnp.dot(activated, w_down, preferred_element_type=jnp.float32).astype(jnp.bfloat16)

    outs = []
    for j in range(full):
        rows = x_recv[:, j].reshape(unit_rows, model_width)
        outs.append(expert_rows(rows, full_in[j], full_out[j], hidden_units))
    for i in range(halves):
        rows = x_recv[:, full + i].reshape(unit_rows, model_width)
        if paired:
            w_down = part_out[i]
        else:
            chunk_at = (dp_at * halves + i) % chunks
            w_down = lax.dynamic_slice_in_dim(
                part_out[i], chunk_at * sources_per_chunk, sources_per_chunk, axis=0
            ).reshape(chunk_width, model_width)
        outs.append(expert_rows(rows, part_in[i], w_down, chunk_width))
    y_send = (
        jnp.stack(outs)
        .reshape(full + halves, n_dp, n_exp, CAP_MOST, model_width)
        .transpose(1, 0, 2, 3, 4)
    )
    weight_hi = weight.astype(jnp.bfloat16)
    weight_lo = (weight - weight_hi.astype(jnp.float32)).astype(jnp.bfloat16)
    halves_d = 2 if model_width % 256 == 0 else 1
    piece_width = model_width // halves_d
    combined_parts = []
    for h in range(halves_d):
        cols = slice(h * piece_width, (h + 1) * piece_width)
        y_recv = lax.all_to_all(y_send[..., cols], "dp", 0, 0, tiled=True)
        slot_out = [None] * slot_local
        for o in range(n_dp):
            for j, s in enumerate(owned_full[o]):
                slot_out[s] = y_recv[o, j]
            for i, (s, _) in enumerate(owned_part[o]):
                part = y_recv[o, full + i].astype(jnp.float32)
                slot_out[s] = part if slot_out[s] is None else slot_out[s] + part
        slot_out = [part.astype(jnp.bfloat16) for part in slot_out]
        expert_out = jnp.stack(slot_out, axis=1).reshape(
            n_exp, slot_local * CAP_MOST, piece_width
        )
        partial = jnp.einsum(
            "btr,brd->btd", weight_hi, expert_out, preferred_element_type=jnp.float32
        ) + jnp.einsum("btr,brd->btd", weight_lo, expert_out, preferred_element_type=jnp.float32)
        combined_parts.append(
            lax.psum_scatter(
                partial.reshape(n_exp * tok_rows, piece_width).astype(jnp.bfloat16),
                "expert",
                scatter_dimension=0,
                tiled=True,
            )
        )
    combined = jnp.concatenate(combined_parts, axis=-1)
    residual_out = (hidden_state.astype(jnp.float32) + combined.astype(jnp.float32)).astype(
        jnp.bfloat16
    )
    next_normed = rms_scale(residual_out, gain_next).astype(jnp.bfloat16)
    return (residual_out, next_normed)


def solution(mesh):
    placed = (
        P("expert", None, None, "dp"),
        P("dp", None),
        P(("dp", "expert"), None),
        P(),
        P(),
        P(),
        P(("dp", "expert"), None),
        P(("dp", "expert"), None),
        P(),
        P(),
        P("expert", "dp", None),
        P("expert", "dp", None),
    )
    return jax.shard_map(
        on_device_body,
        mesh=mesh,
        in_specs=placed,
        out_specs=(P(("dp", "expert"), None), P(("dp", "expert"), None)),
        check_vma=False,
    )
```

```python
import math

import jax
import jax.numpy as jnp
from jax import lax
from jax.sharding import PartitionSpec as P


CAP_UNIT = 8
CAP_MOST = 32


def rms_scale(values, gain):
    widened = values.astype(jnp.float32)
    return widened * lax.rsqrt(jnp.mean(widened * widened, axis=-1, keepdims=True) + 1e-06) * gain


def route_rows(logits, w_router, expert_ids, replica_pick, slot_expert, cap_blocks, cap_unit):
    blocks, row_count, topk_all = expert_ids.shape
    experts_all = w_router.shape[1]
    slots_all = slot_expert.shape[0]
    logits = logits.reshape(blocks, row_count, experts_all)
    expert_axis = jnp.arange(experts_all)
    one_hot = expert_ids[..., None] == expert_axis
    chosen = jnp.sum(jnp.where(one_hot, logits[:, :, None, :], jnp.float32(0.0)), axis=-1)
    raised = jnp.exp(chosen)
    gates = raised / jnp.sum(raised, axis=-1, keepdims=True)
    holder = (slot_expert[None, :] == expert_axis[:, None]).astype(jnp.int32)
    rep_count = jnp.sum(holder, axis=1)
    earlier = jnp.cumsum(holder, axis=1) - holder
    slot_rank = jnp.sum(earlier * holder, axis=0)
    count_of = jnp.sum(jnp.where(one_hot, rep_count, 0), axis=-1)
    replica = replica_pick % count_of
    slot_axis = jnp.arange(slots_all)
    matched = (slot_expert == expert_ids[..., None]) & (slot_rank == replica[..., None])
    target_slot = jnp.sum(jnp.where(matched, slot_axis, 0), axis=-1)
    flat_count = row_count * topk_all
    selected = matched.reshape(blocks, flat_count, slots_all)
    flat_axis = lax.optimization_barrier(jnp.arange(flat_count))
    lower = (flat_axis[:, None] > flat_axis[None, :]).astype(jnp.bfloat16)
    before = jnp.einsum(
        "ij,bjs->bis", lower, selected.astype(jnp.bfloat16), preferred_element_type=jnp.float32
    )
    position = (
        jnp.sum(jnp.where(selected, before, jnp.float32(0.0)), axis=-1)
        .astype(jnp.int32)
        .reshape(blocks, row_count, topk_all)
    )
    capacity = (
        jnp.sum(jnp.where(target_slot[..., None] == slot_axis, cap_blocks, 0), axis=-1) * cap_unit
    )
    retained = position < capacity
    return (gates, target_slot, position, retained)


def unit_plan(slot_local, n_dp, hidden_units):
    full = slot_local // n_dp
    rest = slot_local - full * n_dp
    chunks = n_dp // math.gcd(rest, n_dp) if rest else 1
    halves = rest * chunks // n_dp
    chunk_width = hidden_units // chunks
    owned_full = [[o * full + j for j in range(full)] for o in range(n_dp)]
    if halves == 1 and rest * chunks == n_dp:
        owned_part = [[(full * n_dp + o % rest, o // rest)] for o in range(n_dp)]
    else:
        owned_part = [
            [(full * n_dp + (o * halves + i) // chunks, (o * halves + i) % chunks)
             for i in range(halves)]
            for o in range(n_dp)
        ]
    return full, halves, chunks, chunk_width, owned_full, owned_part


def on_device_body(
    context,
    w_proj,
    residual,
    gain_first,
    gain_next,
    w_router,
    expert_ids,
    replica_pick,
    slot_expert,
    cap_blocks,
    w_in,
    w_out,
):
    tok_rows, model_width = residual.shape
    topk_all = expert_ids.shape[1]
    slot_local, d_local, _ = w_in.shape
    hidden_units = w_in.shape[2] // 2
    ff_local = w_out.shape[1]
    n_dp = lax.axis_size("dp")
    n_exp = lax.axis_size("expert")
    dp_at = lax.axis_index("dp")
    exp_at = lax.axis_index("expert")
    full, halves, chunks, chunk_width, owned_full, owned_part = unit_plan(
        slot_local, n_dp, hidden_units
    )
    sources_per_chunk = chunk_width // ff_local
    rest = slot_local - full * n_dp
    paired = (
        halves == 1 and rest * chunks == n_dp and chunk_width == rest * ff_local
    )
    lane_width = 2 * chunk_width if (ff_local * model_width) % (2 * chunk_width) == 0 else 128

    def as_rows(piece):
        return piece.reshape(-1, lane_width)

    weight_parts = []
    for o in range(n_dp):
        pieces = []
        for s in owned_full[o]:
            pieces += [as_rows(w_in[s]), as_rows(w_out[s])]
        for s, c in owned_part[o]:
            lo = c * chunk_width
            pieces += [
                as_rows(w_in[s, :, lo:lo + chunk_width]),
                as_rows(w_in[s, :, hidden_units + lo:hidden_units + lo + chunk_width]),
            ]
            if not paired:
                pieces.append(as_rows(w_out[s]))
        weight_parts.append(jnp.concatenate(pieces, axis=0))
    weight_send = jnp.stack(weight_parts)
    weight_recv = lax.all_to_all(weight_send, "dp", 0, 0, tiled=True)
    offset = 0


    def take(shape):
        nonlocal offset
        count = math.prod(shape) // lane_width
        piece = weight_recv[:, offset:offset + count].reshape((n_dp,) + shape)
        offset += count
        return piece

    full_in, full_out, part_in, part_out = [], [], [], []
    for _ in range(full):
        full_in.append(take((d_local, 2 * hidden_units)).reshape(n_dp * d_local, 2 * hidden_units))
        full_out.append(take((ff_local, model_width)).reshape(n_dp * ff_local, model_width))
    for _ in range(halves):
        gate_in = take((d_local, chunk_width))
        up_in = take((d_local, chunk_width))
        part_in.append(
            jnp.concatenate([gate_in, up_in], axis=-1).reshape(n_dp * d_local, 2 * chunk_width)
        )
        if not paired:
            part_out.append(take((ff_local, model_width)))
    if paired:
        group_at = dp_at % rest
        held = [lax.dynamic_index_in_dim(w_out, full * n_dp + group_at, 0, keepdims=False)]
        for k in range(1, rest):
            sent = lax.dynamic_index_in_dim(
                w_out, full * n_dp + (group_at + rest - k) % rest, 0, keepdims=False
            )
            pairs = [
                (base + (p + k) % rest, base + p)
                for base in range(0, n_dp, rest)
                for p in range(rest)
            ]
            held.append(lax.ppermute(sent, "dp", pairs))
        part_out.append(
            jnp.roll(jnp.stack(held), group_at, axis=0).reshape(chunk_width, model_width)
        )

    ids_all = lax.all_gather(
        jnp.concatenate([expert_ids, replica_pick], axis=1), "expert", axis=0, tiled=True
    ).reshape(n_exp, tok_rows, 2 * topk_all)

    flat_context = context.reshape(-1, context.shape[3])
    attended = lax.psum_scatter(
        jnp.dot(flat_context, w_proj, preferred_element_type=jnp.float32),
        "dp",
        scatter_dimension=0,
        tiled=True,
    )
    hidden_state = (residual.astype(jnp.float32) + attended.astype(jnp.float32)).astype(
        jnp.bfloat16
    )
    normed = rms_scale(hidden_state, gain_first).astype(jnp.bfloat16)

    normed_all = lax.all_gather(normed, "expert", axis=0, tiled=True)
    logits = jnp.dot(normed_all, w_router, preferred_element_type=jnp.float32)
    gates, target_slot, position, retained = route_rows(
        logits,
        w_router,
        ids_all[:, :, :topk_all],
        ids_all[:, :, topk_all:],
        slot_expert,
        cap_blocks,
        CAP_UNIT,
    )
    here = retained & (target_slot // slot_local == exp_at)
    local = jnp.where(here, (target_slot % slot_local) * CAP_MOST + position, -1)
    hit = local[..., None] == jnp.arange(slot_local * CAP_MOST)
    pick = jnp.any(hit, axis=2).astype(jnp.bfloat16)
    weight = jnp.sum(jnp.where(hit, gates[..., None], jnp.float32(0.0)), axis=2)
    slot_in = jnp.einsum(
        "btr,btd->brd",
        pick,
        normed_all.reshape(n_exp, tok_rows, model_width),
        preferred_element_type=jnp.float32,
    ).astype(jnp.bfloat16)
    slot_in = slot_in.reshape(n_exp, slot_local, CAP_MOST, model_width)

    x_parts = []
    for o in range(n_dp):
        x_parts.append(
            jnp.stack([slot_in[:, s] for s in owned_full[o]] + [slot_in[:, s] for s, _ in owned_part[o]])
        )
    x_recv = lax.all_to_all(jnp.stack(x_parts), "dp", 0, 0, tiled=True)

    unit_rows = n_dp * n_exp * CAP_MOST

    def expert_rows(rows, w_up, w_down, width):
        gate_up = jnp.dot(rows, w_up, preferred_element_type=jnp.float32)
        activated = (jax.nn.silu(gate_up[:, :width]) * gate_up[:, width:]).astype(jnp.bfloat16)
        return jnp.dot(activated, w_down, preferred_element_type=jnp.float32).astype(jnp.bfloat16)

    outs = []
    for j in range(full):
        rows = x_recv[:, j].reshape(unit_rows, model_width)
        outs.append(expert_rows(rows, full_in[j], full_out[j], hidden_units))
    for i in range(halves):
        rows = x_recv[:, full + i].reshape(unit_rows, model_width)
        if paired:
            w_down = part_out[i]
        else:
            chunk_at = (dp_at * halves + i) % chunks
            w_down = lax.dynamic_slice_in_dim(
                part_out[i], chunk_at * sources_per_chunk, sources_per_chunk, axis=0
            ).reshape(chunk_width, model_width)
        outs.append(expert_rows(rows, part_in[i], w_down, chunk_width))
    y_send = (
        jnp.stack(outs)
        .reshape(full + halves, n_dp, n_exp, CAP_MOST, model_width)
        .transpose(1, 0, 2, 3, 4)
    )
    weight_hi = weight.astype(jnp.bfloat16)
    weight_lo = (weight - weight_hi.astype(jnp.float32)).astype(jnp.bfloat16)
    halves_d = 2 if model_width % 256 == 0 else 1
    piece_width = model_width // halves_d
    combined_parts = []
    for h in range(halves_d):
        cols = slice(h * piece_width, (h + 1) * piece_width)
        y_recv = lax.all_to_all(y_send[..., cols], "dp", 0, 0, tiled=True)
        slot_out = [None] * slot_local
        for o in range(n_dp):
            for j, s in enumerate(owned_full[o]):
                slot_out[s] = y_recv[o, j]
            for i, (s, _) in enumerate(owned_part[o]):
                part = y_recv[o, full + i].astype(jnp.float32)
                slot_out[s] = part if slot_out[s] is None else slot_out[s] + part
        slot_out = [part.astype(jnp.bfloat16) for part in slot_out]
        expert_out = jnp.stack(slot_out, axis=1).reshape(
            n_exp, slot_local * CAP_MOST, piece_width
        )
        partial = jnp.einsum(
            "btr,brd->btd", weight_hi, expert_out, preferred_element_type=jnp.float32
        ) + jnp.einsum("btr,brd->btd", weight_lo, expert_out, preferred_element_type=jnp.float32)
        combined_parts.append(
            lax.psum_scatter(
                partial.reshape(n_exp * tok_rows, piece_width).astype(jnp.bfloat16),
                "expert",
                scatter_dimension=0,
                tiled=True,
            )
        )
    combined = jnp.concatenate(combined_parts, axis=-1)
    residual_out = (hidden_state.astype(jnp.float32) + combined.astype(jnp.float32)).astype(
        jnp.bfloat16
    )
    next_normed = rms_scale(residual_out, gain_next).astype(jnp.bfloat16)
    return (residual_out, next_normed)


def solution(mesh):
    placed = (
        P("expert", None, None, "dp"),
        P("dp", None),
        P(("dp", "expert"), None),
        P(),
        P(),
        P(),
        P(("dp", "expert"), None),
        P(("dp", "expert"), None),
        P(),
        P(),
        P("expert", "dp", None),
        P("expert", "dp", None),
    )
    return jax.shard_map(
        on_device_body,
        mesh=mesh,
        in_specs=placed,
        out_specs=(P(("dp", "expert"), None), P(("dp", "expert"), None)),
        check_vma=False,
    )
```

```python
import math

import jax
import jax.numpy as jnp
from jax import lax
from jax.sharding import PartitionSpec as P


CAP_UNIT = 8
CAP_MOST = 32


def rms_scale(values, gain):
    widened = values.astype(jnp.float32)
    return widened * lax.rsqrt(jnp.mean(widened * widened, axis=-1, keepdims=True) + 1e-06) * gain


def route_rows(logits, w_router, expert_ids, replica_pick, slot_expert, cap_blocks, cap_unit):
    blocks, row_count, topk_all = expert_ids.shape
    experts_all = w_router.shape[1]
    slots_all = slot_expert.shape[0]
    logits = logits.reshape(blocks, row_count, experts_all)
    expert_axis = jnp.arange(experts_all)
    one_hot = expert_ids[..., None] == expert_axis
    chosen = jnp.sum(jnp.where(one_hot, logits[:, :, None, :], jnp.float32(0.0)), axis=-1)
    raised = jnp.exp(chosen)
    gates = raised / jnp.sum(raised, axis=-1, keepdims=True)
    holder = (slot_expert[None, :] == expert_axis[:, None]).astype(jnp.int32)
    rep_count = jnp.sum(holder, axis=1)
    earlier = jnp.cumsum(holder, axis=1) - holder
    slot_rank = jnp.sum(earlier * holder, axis=0)
    count_of = jnp.sum(jnp.where(one_hot, rep_count, 0), axis=-1)
    replica = replica_pick % count_of
    slot_axis = jnp.arange(slots_all)
    matched = (slot_expert == expert_ids[..., None]) & (slot_rank == replica[..., None])
    target_slot = jnp.sum(jnp.where(matched, slot_axis, 0), axis=-1)
    flat_count = row_count * topk_all
    selected = matched.reshape(blocks, flat_count, slots_all)
    flat_axis = lax.optimization_barrier(jnp.arange(flat_count))
    lower = (flat_axis[:, None] > flat_axis[None, :]).astype(jnp.bfloat16)
    before = jnp.einsum(
        "ij,bjs->bis", lower, selected.astype(jnp.bfloat16), preferred_element_type=jnp.float32
    )
    position = (
        jnp.sum(jnp.where(selected, before, jnp.float32(0.0)), axis=-1)
        .astype(jnp.int32)
        .reshape(blocks, row_count, topk_all)
    )
    capacity = (
        jnp.sum(jnp.where(target_slot[..., None] == slot_axis, cap_blocks, 0), axis=-1) * cap_unit
    )
    retained = position < capacity
    return (gates, target_slot, position, retained)


def unit_plan(slot_local, n_dp, hidden_units):
    full = slot_local // n_dp
    rest = slot_local - full * n_dp
    chunks = n_dp // math.gcd(rest, n_dp) if rest else 1
    halves = rest * chunks // n_dp
    chunk_width = hidden_units // chunks
    owned_full = [[o * full + j for j in range(full)] for o in range(n_dp)]
    if halves == 1 and rest * chunks == n_dp:
        owned_part = [[(full * n_dp + o % rest, o // rest)] for o in range(n_dp)]
    else:
        owned_part = [
            [(full * n_dp + (o * halves + i) // chunks, (o * halves + i) % chunks)
             for i in range(halves)]
            for o in range(n_dp)
        ]
    return full, halves, chunks, chunk_width, owned_full, owned_part


def on_device_body(
    context,
    w_proj,
    residual,
    gain_first,
    gain_next,
    w_router,
    expert_ids,
    replica_pick,
    slot_expert,
    cap_blocks,
    w_in,
    w_out,
):
    tok_rows, model_width = residual.shape
    topk_all = expert_ids.shape[1]
    slot_local, d_local, _ = w_in.shape
    hidden_units = w_in.shape[2] // 2
    ff_local = w_out.shape[1]
    n_dp = lax.axis_size("dp")
    n_exp = lax.axis_size("expert")
    dp_at = lax.axis_index("dp")
    exp_at = lax.axis_index("expert")
    full, halves, chunks, chunk_width, owned_full, owned_part = unit_plan(
        slot_local, n_dp, hidden_units
    )
    sources_per_chunk = chunk_width // ff_local
    rest = slot_local - full * n_dp
    paired = (
        halves == 1 and rest * chunks == n_dp and chunk_width == rest * ff_local
    )
    lane_width = 2 * chunk_width if (ff_local * model_width) % (2 * chunk_width) == 0 else 128

    def as_rows(piece):
        return piece.reshape(-1, lane_width)

    weight_parts = []
    for o in range(n_dp):
        pieces = []
        for s in owned_full[o]:
            pieces += [as_rows(w_in[s]), as_rows(w_out[s])]
        for s, c in owned_part[o]:
            lo = c * chunk_width
            pieces += [
                as_rows(w_in[s, :, lo:lo + chunk_width]),
                as_rows(w_in[s, :, hidden_units + lo:hidden_units + lo + chunk_width]),
            ]
            if not paired:
                pieces.append(as_rows(w_out[s]))
        weight_parts.append(jnp.concatenate(pieces, axis=0))
    weight_send = jnp.stack(weight_parts)
    weight_recv = lax.all_to_all(weight_send, "dp", 0, 0, tiled=True)
    offset = 0


    def take(shape):
        nonlocal offset
        count = math.prod(shape) // lane_width
        piece = weight_recv[:, offset:offset + count].reshape((n_dp,) + shape)
        offset += count
        return piece

    full_in, full_out, part_in, part_out = [], [], [], []
    for _ in range(full):
        full_in.append(take((d_local, 2 * hidden_units)).reshape(n_dp * d_local, 2 * hidden_units))
        full_out.append(take((ff_local, model_width)).reshape(n_dp * ff_local, model_width))
    for _ in range(halves):
        gate_in = take((d_local, chunk_width))
        up_in = take((d_local, chunk_width))
        part_in.append(
            jnp.concatenate([gate_in, up_in], axis=-1).reshape(n_dp * d_local, 2 * chunk_width)
        )
        if not paired:
            part_out.append(take((ff_local, model_width)))
    if paired:
        group_at = dp_at % rest
        held = [lax.dynamic_index_in_dim(w_out, full * n_dp + group_at, 0, keepdims=False)]
        for k in range(1, rest):
            sent = lax.dynamic_index_in_dim(
                w_out, full * n_dp + (group_at + rest - k) % rest, 0, keepdims=False
            )
            pairs = [
                (base + (p + k) % rest, base + p)
                for base in range(0, n_dp, rest)
                for p in range(rest)
            ]
            held.append(lax.ppermute(sent, "dp", pairs))
        part_out.append(
            jnp.roll(jnp.stack(held), group_at, axis=0).reshape(chunk_width, model_width)
        )

    ids_all = lax.all_gather(
        jnp.concatenate([expert_ids, replica_pick], axis=1), "expert", axis=0, tiled=True
    ).reshape(n_exp, tok_rows, 2 * topk_all)

    flat_context = context.reshape(-1, context.shape[3])
    head_parts = jnp.dot(flat_context, w_proj, preferred_element_type=jnp.float32)
    head_parts = lax.all_to_all(
        head_parts.reshape(n_dp, tok_rows, model_width), "dp", 0, 0, tiled=True
    )
    attended = jnp.sum(head_parts, axis=0)
    hidden_state = (residual.astype(jnp.float32) + attended.astype(jnp.float32)).astype(
        jnp.bfloat16
    )
    normed = rms_scale(hidden_state, gain_first).astype(jnp.bfloat16)

    normed_all = lax.all_gather(normed, "expert", axis=0, tiled=True)
    logits = jnp.dot(normed_all, w_router, preferred_element_type=jnp.float32)
    gates, target_slot, position, retained = route_rows(
        logits,
        w_router,
        ids_all[:, :, :topk_all],
        ids_all[:, :, topk_all:],
        slot_expert,
        cap_blocks,
        CAP_UNIT,
    )
    here = retained & (target_slot // slot_local == exp_at)
    local = jnp.where(here, (target_slot % slot_local) * CAP_MOST + position, -1)
    hit = local[..., None] == jnp.arange(slot_local * CAP_MOST)
    pick = jnp.any(hit, axis=2).astype(jnp.bfloat16)
    weight = jnp.sum(jnp.where(hit, gates[..., None], jnp.float32(0.0)), axis=2)
    slot_in = jnp.einsum(
        "btr,btd->brd",
        pick,
        normed_all.reshape(n_exp, tok_rows, model_width),
        preferred_element_type=jnp.float32,
    ).astype(jnp.bfloat16)
    slot_in = slot_in.reshape(n_exp, slot_local, CAP_MOST, model_width)

    x_parts = []
    for o in range(n_dp):
        x_parts.append(
            jnp.stack([slot_in[:, s] for s in owned_full[o]] + [slot_in[:, s] for s, _ in owned_part[o]])
        )
    x_recv = lax.all_to_all(jnp.stack(x_parts), "dp", 0, 0, tiled=True)

    unit_rows = n_dp * n_exp * CAP_MOST

    def expert_rows(rows, w_up, w_down, width):
        gate_up = jnp.dot(rows, w_up, preferred_element_type=jnp.float32)
        activated = (jax.nn.silu(gate_up[:, :width]) * gate_up[:, width:]).astype(jnp.bfloat16)
        return jnp.dot(activated, w_down, preferred_element_type=jnp.float32).astype(jnp.bfloat16)

    outs = []
    for j in range(full):
        rows = x_recv[:, j].reshape(unit_rows, model_width)
        outs.append(expert_rows(rows, full_in[j], full_out[j], hidden_units))
    for i in range(halves):
        rows = x_recv[:, full + i].reshape(unit_rows, model_width)
        if paired:
            w_down = part_out[i]
        else:
            chunk_at = (dp_at * halves + i) % chunks
            w_down = lax.dynamic_slice_in_dim(
                part_out[i], chunk_at * sources_per_chunk, sources_per_chunk, axis=0
            ).reshape(chunk_width, model_width)
        outs.append(expert_rows(rows, part_in[i], w_down, chunk_width))
    y_send = (
        jnp.stack(outs)
        .reshape(full + halves, n_dp, n_exp, CAP_MOST, model_width)
        .transpose(1, 0, 2, 3, 4)
    )
    weight_hi = weight.astype(jnp.bfloat16)
    weight_lo = (weight - weight_hi.astype(jnp.float32)).astype(jnp.bfloat16)
    halves_d = 2 if model_width % 256 == 0 else 1
    piece_width = model_width // halves_d
    combined_parts = []
    for h in range(halves_d):
        cols = slice(h * piece_width, (h + 1) * piece_width)
        y_recv = lax.all_to_all(y_send[..., cols], "dp", 0, 0, tiled=True)
        slot_out = [None] * slot_local
        for o in range(n_dp):
            for j, s in enumerate(owned_full[o]):
                slot_out[s] = y_recv[o, j]
            for i, (s, _) in enumerate(owned_part[o]):
                part = y_recv[o, full + i].astype(jnp.float32)
                slot_out[s] = part if slot_out[s] is None else slot_out[s] + part
        slot_out = [part.astype(jnp.bfloat16) for part in slot_out]
        expert_out = jnp.stack(slot_out, axis=1).reshape(
            n_exp, slot_local * CAP_MOST, piece_width
        )
        partial = jnp.einsum(
            "btr,brd->btd", weight_hi, expert_out, preferred_element_type=jnp.float32
        ) + jnp.einsum("btr,brd->btd", weight_lo, expert_out, preferred_element_type=jnp.float32)
        combined_parts.append(
            lax.psum_scatter(
                partial.reshape(n_exp * tok_rows, piece_width).astype(jnp.bfloat16),
                "expert",
                scatter_dimension=0,
                tiled=True,
            )
        )
    combined = jnp.concatenate(combined_parts, axis=-1)
    residual_out = (hidden_state.astype(jnp.float32) + combined.astype(jnp.float32)).astype(
        jnp.bfloat16
    )
    next_normed = rms_scale(residual_out, gain_next).astype(jnp.bfloat16)
    return (residual_out, next_normed)


def solution(mesh):
    placed = (
        P("expert", None, None, "dp"),
        P("dp", None),
        P(("dp", "expert"), None),
        P(),
        P(),
        P(),
        P(("dp", "expert"), None),
        P(("dp", "expert"), None),
        P(),
        P(),
        P("expert", "dp", None),
        P("expert", "dp", None),
    )
    return jax.shard_map(
        on_device_body,
        mesh=mesh,
        in_specs=placed,
        out_specs=(P(("dp", "expert"), None), P(("dp", "expert"), None)),
        check_vma=False,
    )
```

```python
import math

import jax
import jax.numpy as jnp
from jax import lax
from jax.sharding import PartitionSpec as P


CAP_UNIT = 8
CAP_MOST = 32


def rms_scale(values, gain):
    widened = values.astype(jnp.float32)
    return widened * lax.rsqrt(jnp.mean(widened * widened, axis=-1, keepdims=True) + 1e-06) * gain


def route_rows(logits, w_router, expert_ids, replica_pick, slot_expert, cap_blocks, cap_unit):
    blocks, row_count, topk_all = expert_ids.shape
    experts_all = w_router.shape[1]
    slots_all = slot_expert.shape[0]
    logits = logits.reshape(blocks, row_count, experts_all)
    expert_axis = jnp.arange(experts_all)
    one_hot = expert_ids[..., None] == expert_axis
    chosen = jnp.sum(jnp.where(one_hot, logits[:, :, None, :], jnp.float32(0.0)), axis=-1)
    raised = jnp.exp(chosen)
    gates = raised / jnp.sum(raised, axis=-1, keepdims=True)
    holder = (slot_expert[None, :] == expert_axis[:, None]).astype(jnp.int32)
    rep_count = jnp.sum(holder, axis=1)
    earlier = jnp.cumsum(holder, axis=1) - holder
    slot_rank = jnp.sum(earlier * holder, axis=0)
    count_of = jnp.sum(jnp.where(one_hot, rep_count, 0), axis=-1)
    replica = replica_pick % count_of
    slot_axis = jnp.arange(slots_all)
    matched = (slot_expert == expert_ids[..., None]) & (slot_rank == replica[..., None])
    target_slot = jnp.sum(jnp.where(matched, slot_axis, 0), axis=-1)
    flat_count = row_count * topk_all
    selected = matched.reshape(blocks, flat_count, slots_all)
    flat_axis = lax.optimization_barrier(jnp.arange(flat_count))
    lower = (flat_axis[:, None] > flat_axis[None, :]).astype(jnp.bfloat16)
    before = jnp.einsum(
        "ij,bjs->bis", lower, selected.astype(jnp.bfloat16), preferred_element_type=jnp.float32
    )
    position = (
        jnp.sum(jnp.where(selected, before, jnp.float32(0.0)), axis=-1)
        .astype(jnp.int32)
        .reshape(blocks, row_count, topk_all)
    )
    capacity = (
        jnp.sum(jnp.where(target_slot[..., None] == slot_axis, cap_blocks, 0), axis=-1) * cap_unit
    )
    retained = position < capacity
    return (gates, target_slot, position, retained)


def unit_plan(slot_local, n_dp, hidden_units):
    full = slot_local // n_dp
    rest = slot_local - full * n_dp
    chunks = n_dp // math.gcd(rest, n_dp) if rest else 1
    halves = rest * chunks // n_dp
    chunk_width = hidden_units // chunks
    owned_full = [[o * full + j for j in range(full)] for o in range(n_dp)]
    if halves == 1 and rest * chunks == n_dp:
        owned_part = [[(full * n_dp + o % rest, o // rest)] for o in range(n_dp)]
    else:
        owned_part = [
            [(full * n_dp + (o * halves + i) // chunks, (o * halves + i) % chunks)
             for i in range(halves)]
            for o in range(n_dp)
        ]
    return full, halves, chunks, chunk_width, owned_full, owned_part


def on_device_body(
    context,
    w_proj,
    residual,
    gain_first,
    gain_next,
    w_router,
    expert_ids,
    replica_pick,
    slot_expert,
    cap_blocks,
    w_in,
    w_out,
):
    tok_rows, model_width = residual.shape
    topk_all = expert_ids.shape[1]
    slot_local, d_local, _ = w_in.shape
    hidden_units = w_in.shape[2] // 2
    ff_local = w_out.shape[1]
    n_dp = lax.axis_size("dp")
    n_exp = lax.axis_size("expert")
    dp_at = lax.axis_index("dp")
    exp_at = lax.axis_index("expert")
    full, halves, chunks, chunk_width, owned_full, owned_part = unit_plan(
        slot_local, n_dp, hidden_units
    )
    sources_per_chunk = chunk_width // ff_local
    rest = slot_local - full * n_dp
    paired = (
        halves == 1 and rest * chunks == n_dp and chunk_width == rest * ff_local
    )
    lane_width = 2 * chunk_width if (ff_local * model_width) % (2 * chunk_width) == 0 else 128

    def as_rows(piece):
        return piece.reshape(-1, lane_width)

    weight_parts = []
    for o in range(n_dp):
        pieces = []
        for s in owned_full[o]:
            pieces += [as_rows(w_in[s]), as_rows(w_out[s])]
        for s, c in owned_part[o]:
            lo = c * chunk_width
            pieces += [
                as_rows(w_in[s, :, lo:lo + chunk_width]),
                as_rows(w_in[s, :, hidden_units + lo:hidden_units + lo + chunk_width]),
            ]
            if not paired:
                pieces.append(as_rows(w_out[s]))
        weight_parts.append(jnp.concatenate(pieces, axis=0))
    weight_send = jnp.stack(weight_parts)
    weight_recv = lax.all_to_all(weight_send, "dp", 0, 0, tiled=True)
    offset = 0


    def take(shape):
        nonlocal offset
        count = math.prod(shape) // lane_width
        piece = weight_recv[:, offset:offset + count].reshape((n_dp,) + shape)
        offset += count
        return piece

    full_in, full_out, part_in, part_out = [], [], [], []
    for _ in range(full):
        full_in.append(take((d_local, 2 * hidden_units)).reshape(n_dp * d_local, 2 * hidden_units))
        full_out.append(take((ff_local, model_width)).reshape(n_dp * ff_local, model_width))
    for _ in range(halves):
        gate_in = take((d_local, chunk_width))
        up_in = take((d_local, chunk_width))
        part_in.append(
            jnp.concatenate([gate_in, up_in], axis=-1).reshape(n_dp * d_local, 2 * chunk_width)
        )
        if not paired:
            part_out.append(take((ff_local, model_width)))
    if paired:
        group_at = dp_at % rest
        held = [lax.dynamic_index_in_dim(w_out, full * n_dp + group_at, 0, keepdims=False)]
        for k in range(1, rest):
            sent = lax.dynamic_index_in_dim(
                w_out, full * n_dp + (group_at + rest - k) % rest, 0, keepdims=False
            )
            pairs = [
                (base + (p + k) % rest, base + p)
                for base in range(0, n_dp, rest)
                for p in range(rest)
            ]
            held.append(lax.ppermute(sent, "dp", pairs))
        part_out.append(
            jnp.roll(jnp.stack(held), group_at, axis=0).reshape(chunk_width, model_width)
        )

    ids_all = lax.all_gather(
        jnp.concatenate([expert_ids, replica_pick], axis=1), "expert", axis=0, tiled=True
    ).reshape(n_exp, tok_rows, 2 * topk_all)

    flat_context = context.reshape(-1, context.shape[3])
    head_parts = jnp.dot(flat_context, w_proj, preferred_element_type=jnp.float32)
    head_parts = lax.all_to_all(
        head_parts.reshape(n_dp, tok_rows, model_width), "dp", 0, 0, tiled=True
    )
    attended = jnp.sum(head_parts, axis=0)
    hidden_state = (residual.astype(jnp.float32) + attended.astype(jnp.float32)).astype(
        jnp.bfloat16
    )
    normed = rms_scale(hidden_state, gain_first).astype(jnp.bfloat16)

    normed_all = lax.all_gather(normed, "expert", axis=0, tiled=True)
    logits = jnp.dot(normed_all, w_router, preferred_element_type=jnp.float32)
    gates, target_slot, position, retained = route_rows(
        logits,
        w_router,
        ids_all[:, :, :topk_all],
        ids_all[:, :, topk_all:],
        slot_expert,
        cap_blocks,
        CAP_UNIT,
    )
    here = retained & (target_slot // slot_local == exp_at)
    local = jnp.where(here, (target_slot % slot_local) * CAP_MOST + position, -1)
    hit = local[..., None] == jnp.arange(slot_local * CAP_MOST)
    pick = jnp.any(hit, axis=2).astype(jnp.bfloat16)
    weight = jnp.sum(jnp.where(hit, gates[..., None], jnp.float32(0.0)), axis=2)
    slot_in = jnp.einsum(
        "btr,btd->brd",
        pick,
        normed_all.reshape(n_exp, tok_rows, model_width),
        preferred_element_type=jnp.float32,
    ).astype(jnp.bfloat16)
    slot_in = slot_in.reshape(n_exp, slot_local, CAP_MOST, model_width)

    x_parts = []
    for o in range(n_dp):
        x_parts.append(
            jnp.stack([slot_in[:, s] for s in owned_full[o]] + [slot_in[:, s] for s, _ in owned_part[o]])
        )
    x_send = jnp.stack(x_parts)
    src_pieces = 2 if n_exp % 2 == 0 else 1
    src_width = n_exp // src_pieces
    x_recvs = [
        lax.all_to_all(x_send[:, :, p * src_width:(p + 1) * src_width], "dp", 0, 0, tiled=True)
        for p in range(src_pieces)
    ]

    piece_rows = n_dp * src_width * CAP_MOST

    def activate(rows, w_up, width):
        gate_up = jnp.dot(rows, w_up, preferred_element_type=jnp.float32)
        return (jax.nn.silu(gate_up[:, :width]) * gate_up[:, width:]).astype(jnp.bfloat16)

    acts, downs = [], []
    for j in range(full):
        acts.append([
            activate(x_recv[:, j].reshape(piece_rows, model_width), full_in[j], hidden_units)
            for x_recv in x_recvs
        ])
        downs.append(full_out[j])
    for i in range(halves):
        if paired:
            w_down = part_out[i]
        else:
            chunk_at = (dp_at * halves + i) % chunks
            w_down = lax.dynamic_slice_in_dim(
                part_out[i], chunk_at * sources_per_chunk, sources_per_chunk, axis=0
            ).reshape(chunk_width, model_width)
        acts.append([
            activate(
                x_recv[:, full + i].reshape(piece_rows, model_width), part_in[i], chunk_width
            )
            for x_recv in x_recvs
        ])
        downs.append(w_down)

    def returned_piece(cols):
        outs = [
            jnp.concatenate(
                [
                    jnp.dot(act, down[:, cols], preferred_element_type=jnp.float32)
                    .astype(jnp.bfloat16)
                    .reshape(n_dp, src_width, CAP_MOST, -1)
                    for act in unit_acts
                ],
                axis=1,
            )
            for unit_acts, down in zip(acts, downs)
        ]
        return jnp.stack(outs, axis=1)

    weight_hi = weight.astype(jnp.bfloat16)
    weight_lo = (weight - weight_hi.astype(jnp.float32)).astype(jnp.bfloat16)
    halves_d = 2 if model_width % 256 == 0 else 1
    piece_width = model_width // halves_d
    combined_parts = []
    for h in range(halves_d):
        cols = slice(h * piece_width, (h + 1) * piece_width)
        y_recv = lax.all_to_all(returned_piece(cols), "dp", 0, 0, tiled=True)
        slot_out = [None] * slot_local
        for o in range(n_dp):
            for j, s in enumerate(owned_full[o]):
                slot_out[s] = y_recv[o, j]
            for i, (s, _) in enumerate(owned_part[o]):
                part = y_recv[o, full + i].astype(jnp.float32)
                slot_out[s] = part if slot_out[s] is None else slot_out[s] + part
        slot_out = [part.astype(jnp.bfloat16) for part in slot_out]
        expert_out = jnp.stack(slot_out, axis=1).reshape(
            n_exp, slot_local * CAP_MOST, piece_width
        )
        partial = jnp.einsum(
            "btr,brd->btd", weight_hi, expert_out, preferred_element_type=jnp.float32
        ) + jnp.einsum("btr,brd->btd", weight_lo, expert_out, preferred_element_type=jnp.float32)
        combined_parts.append(
            lax.psum_scatter(
                partial.reshape(n_exp * tok_rows, piece_width).astype(jnp.bfloat16),
                "expert",
                scatter_dimension=0,
                tiled=True,
            )
        )
    combined = jnp.concatenate(combined_parts, axis=-1)
    residual_out = (hidden_state.astype(jnp.float32) + combined.astype(jnp.float32)).astype(
        jnp.bfloat16
    )
    next_normed = rms_scale(residual_out, gain_next).astype(jnp.bfloat16)
    return (residual_out, next_normed)


def solution(mesh):
    placed = (
        P("expert", None, None, "dp"),
        P("dp", None),
        P(("dp", "expert"), None),
        P(),
        P(),
        P(),
        P(("dp", "expert"), None),
        P(("dp", "expert"), None),
        P(),
        P(),
        P("expert", "dp", None),
        P("expert", "dp", None),
    )
    return jax.shard_map(
        on_device_body,
        mesh=mesh,
        in_specs=placed,
        out_specs=(P(("dp", "expert"), None), P(("dp", "expert"), None)),
        check_vma=False,
    )
```

```python
import math

import jax
import jax.numpy as jnp
from jax import lax
from jax.sharding import PartitionSpec as P


CAP_UNIT = 8
CAP_MOST = 32


def rms_scale(values, gain):
    widened = values.astype(jnp.float32)
    return widened * lax.rsqrt(jnp.mean(widened * widened, axis=-1, keepdims=True) + 1e-06) * gain


def route_rows(logits, w_router, expert_ids, replica_pick, slot_expert, cap_blocks, cap_unit):
    blocks, row_count, topk_all = expert_ids.shape
    experts_all = w_router.shape[1]
    slots_all = slot_expert.shape[0]
    logits = logits.reshape(blocks, row_count, experts_all)
    expert_axis = jnp.arange(experts_all)
    one_hot = expert_ids[..., None] == expert_axis
    chosen = jnp.sum(jnp.where(one_hot, logits[:, :, None, :], jnp.float32(0.0)), axis=-1)
    raised = jnp.exp(chosen)
    gates = raised / jnp.sum(raised, axis=-1, keepdims=True)
    holder = (slot_expert[None, :] == expert_axis[:, None]).astype(jnp.int32)
    rep_count = jnp.sum(holder, axis=1)
    earlier = jnp.cumsum(holder, axis=1) - holder
    slot_rank = jnp.sum(earlier * holder, axis=0)
    count_of = jnp.sum(jnp.where(one_hot, rep_count, 0), axis=-1)
    replica = replica_pick % count_of
    slot_axis = jnp.arange(slots_all)
    matched = (slot_expert == expert_ids[..., None]) & (slot_rank == replica[..., None])
    target_slot = jnp.sum(jnp.where(matched, slot_axis, 0), axis=-1)
    flat_count = row_count * topk_all
    selected = matched.reshape(blocks, flat_count, slots_all)
    flat_axis = lax.optimization_barrier(jnp.arange(flat_count))
    lower = (flat_axis[:, None] > flat_axis[None, :]).astype(jnp.bfloat16)
    before = jnp.einsum(
        "ij,bjs->bis", lower, selected.astype(jnp.bfloat16), preferred_element_type=jnp.float32
    )
    position = (
        jnp.sum(jnp.where(selected, before, jnp.float32(0.0)), axis=-1)
        .astype(jnp.int32)
        .reshape(blocks, row_count, topk_all)
    )
    capacity = (
        jnp.sum(jnp.where(target_slot[..., None] == slot_axis, cap_blocks, 0), axis=-1) * cap_unit
    )
    retained = position < capacity
    return (gates, target_slot, position, retained)


def unit_plan(slot_local, n_dp, hidden_units):
    full = slot_local // n_dp
    rest = slot_local - full * n_dp
    chunks = n_dp // math.gcd(rest, n_dp) if rest else 1
    halves = rest * chunks // n_dp
    chunk_width = hidden_units // chunks
    owned_full = [[o * full + j for j in range(full)] for o in range(n_dp)]
    if halves == 1 and rest * chunks == n_dp:
        owned_part = [[(full * n_dp + o % rest, o // rest)] for o in range(n_dp)]
    else:
        owned_part = [
            [(full * n_dp + (o * halves + i) // chunks, (o * halves + i) % chunks)
             for i in range(halves)]
            for o in range(n_dp)
        ]
    return full, halves, chunks, chunk_width, owned_full, owned_part


def on_device_body(
    context,
    w_proj,
    residual,
    gain_first,
    gain_next,
    w_router,
    expert_ids,
    replica_pick,
    slot_expert,
    cap_blocks,
    w_in,
    w_out,
):
    tok_rows, model_width = residual.shape
    topk_all = expert_ids.shape[1]
    slot_local, d_local, _ = w_in.shape
    hidden_units = w_in.shape[2] // 2
    ff_local = w_out.shape[1]
    n_dp = lax.axis_size("dp")
    n_exp = lax.axis_size("expert")
    dp_at = lax.axis_index("dp")
    exp_at = lax.axis_index("expert")
    full, halves, chunks, chunk_width, owned_full, owned_part = unit_plan(
        slot_local, n_dp, hidden_units
    )
    sources_per_chunk = chunk_width // ff_local
    rest = slot_local - full * n_dp
    paired = (
        halves == 1 and rest * chunks == n_dp and chunk_width == rest * ff_local
    )
    lane_width = 2 * chunk_width if (ff_local * model_width) % (2 * chunk_width) == 0 else 128

    def as_rows(piece):
        return piece.reshape(-1, lane_width)

    weight_parts = []
    for o in range(n_dp):
        pieces = []
        for s in owned_full[o]:
            pieces += [as_rows(w_in[s]), as_rows(w_out[s])]
        for s, c in owned_part[o]:
            lo = c * chunk_width
            pieces += [
                as_rows(w_in[s, :, lo:lo + chunk_width]),
                as_rows(w_in[s, :, hidden_units + lo:hidden_units + lo + chunk_width]),
            ]
            if not paired:
                pieces.append(as_rows(w_out[s]))
        weight_parts.append(jnp.concatenate(pieces, axis=0))
    weight_send = jnp.stack(weight_parts)
    weight_recv = lax.all_to_all(weight_send, "dp", 0, 0, tiled=True)
    offset = 0


    def take(shape):
        nonlocal offset
        count = math.prod(shape) // lane_width
        piece = weight_recv[:, offset:offset + count].reshape((n_dp,) + shape)
        offset += count
        return piece

    full_in, full_out, part_in, part_out = [], [], [], []
    for _ in range(full):
        full_in.append(take((d_local, 2 * hidden_units)).reshape(n_dp * d_local, 2 * hidden_units))
        full_out.append(take((ff_local, model_width)).reshape(n_dp * ff_local, model_width))
    for _ in range(halves):
        gate_in = take((d_local, chunk_width))
        up_in = take((d_local, chunk_width))
        part_in.append(
            jnp.concatenate([gate_in, up_in], axis=-1).reshape(n_dp * d_local, 2 * chunk_width)
        )
        if not paired:
            part_out.append(take((ff_local, model_width)))
    if paired:
        group_at = dp_at % rest
        held = [lax.dynamic_index_in_dim(w_out, full * n_dp + group_at, 0, keepdims=False)]
        for k in range(1, rest):
            sent = lax.dynamic_index_in_dim(
                w_out, full * n_dp + (group_at + rest - k) % rest, 0, keepdims=False
            )
            pairs = [
                (base + (p + k) % rest, base + p)
                for base in range(0, n_dp, rest)
                for p in range(rest)
            ]
            held.append(lax.ppermute(sent, "dp", pairs))
        part_out.append(
            jnp.roll(jnp.stack(held), group_at, axis=0).reshape(chunk_width, model_width)
        )

    ids_all = lax.all_gather(
        jnp.concatenate([expert_ids, replica_pick], axis=1), "expert", axis=0, tiled=True
    ).reshape(n_exp, tok_rows, 2 * topk_all)

    flat_context = context.reshape(-1, context.shape[3])
    head_parts = jnp.dot(flat_context, w_proj, preferred_element_type=jnp.float32)
    split_at = model_width // 2 if model_width % 256 == 0 else model_width
    attended_lo = lax.psum_scatter(
        head_parts[:, :split_at], "dp", scatter_dimension=0, tiled=True
    )
    parts = [attended_lo]
    if split_at < model_width:
        swapped = lax.all_to_all(
            head_parts[:, split_at:].reshape(n_dp, tok_rows, model_width - split_at),
            "dp",
            0,
            0,
            tiled=True,
        )
        parts.append(jnp.sum(swapped, axis=0))
    attended = jnp.concatenate(parts, axis=-1)
    hidden_state = (residual.astype(jnp.float32) + attended.astype(jnp.float32)).astype(
        jnp.bfloat16
    )
    normed = rms_scale(hidden_state, gain_first).astype(jnp.bfloat16)

    normed_all = lax.all_gather(normed, "expert", axis=0, tiled=True)
    logits = jnp.dot(normed_all, w_router, preferred_element_type=jnp.float32)
    gates, target_slot, position, retained = route_rows(
        logits,
        w_router,
        ids_all[:, :, :topk_all],
        ids_all[:, :, topk_all:],
        slot_expert,
        cap_blocks,
        CAP_UNIT,
    )
    here = retained & (target_slot // slot_local == exp_at)
    local = jnp.where(here, (target_slot % slot_local) * CAP_MOST + position, -1)
    hit = local[..., None] == jnp.arange(slot_local * CAP_MOST)
    pick = jnp.any(hit, axis=2).astype(jnp.bfloat16)
    weight = jnp.sum(jnp.where(hit, gates[..., None], jnp.float32(0.0)), axis=2)
    slot_in = jnp.einsum(
        "btr,btd->brd",
        pick,
        normed_all.reshape(n_exp, tok_rows, model_width),
        preferred_element_type=jnp.float32,
    ).astype(jnp.bfloat16)
    slot_in = slot_in.reshape(n_exp, slot_local, CAP_MOST, model_width)

    x_parts = []
    for o in range(n_dp):
        x_parts.append(
            jnp.stack([slot_in[:, s] for s in owned_full[o]] + [slot_in[:, s] for s, _ in owned_part[o]])
        )
    x_recv = lax.all_to_all(jnp.stack(x_parts), "dp", 0, 0, tiled=True)

    unit_rows = n_dp * n_exp * CAP_MOST

    def activate(rows, w_up, width):
        gate_up = jnp.dot(rows, w_up, preferred_element_type=jnp.float32)
        return (jax.nn.silu(gate_up[:, :width]) * gate_up[:, width:]).astype(jnp.bfloat16)

    acts, downs = [], []
    for j in range(full):
        rows = x_recv[:, j].reshape(unit_rows, model_width)
        acts.append(activate(rows, full_in[j], hidden_units))
        downs.append(full_out[j])
    for i in range(halves):
        rows = x_recv[:, full + i].reshape(unit_rows, model_width)
        if paired:
            w_down = part_out[i]
        else:
            chunk_at = (dp_at * halves + i) % chunks
            w_down = lax.dynamic_slice_in_dim(
                part_out[i], chunk_at * sources_per_chunk, sources_per_chunk, axis=0
            ).reshape(chunk_width, model_width)
        acts.append(activate(rows, part_in[i], chunk_width))
        downs.append(w_down)

    def returned_piece(cols):
        outs = [
            jnp.dot(act, down[:, cols], preferred_element_type=jnp.float32)
            .astype(jnp.bfloat16)
            .reshape(n_dp, n_exp, CAP_MOST, -1)
            for act, down in zip(acts, downs)
        ]
        return jnp.stack(outs, axis=1)

    weight_hi = weight.astype(jnp.bfloat16)
    weight_lo = (weight - weight_hi.astype(jnp.float32)).astype(jnp.bfloat16)
    halves_d = 2 if model_width % 256 == 0 else 1
    piece_width = model_width // halves_d
    combined_parts = []
    for h in range(halves_d):
        cols = slice(h * piece_width, (h + 1) * piece_width)
        y_recv = lax.all_to_all(returned_piece(cols), "dp", 0, 0, tiled=True)
        slot_out = [None] * slot_local
        for o in range(n_dp):
            for j, s in enumerate(owned_full[o]):
                slot_out[s] = y_recv[o, j]
            for i, (s, _) in enumerate(owned_part[o]):
                part = y_recv[o, full + i].astype(jnp.float32)
                slot_out[s] = part if slot_out[s] is None else slot_out[s] + part
        slot_out = [part.astype(jnp.bfloat16) for part in slot_out]
        expert_out = jnp.stack(slot_out, axis=1).reshape(
            n_exp, slot_local * CAP_MOST, piece_width
        )
        partial = jnp.einsum(
            "btr,brd->btd", weight_hi, expert_out, preferred_element_type=jnp.float32
        ) + jnp.einsum("btr,brd->btd", weight_lo, expert_out, preferred_element_type=jnp.float32)
        combined_parts.append(
            lax.psum_scatter(
                partial.reshape(n_exp * tok_rows, piece_width).astype(jnp.bfloat16),
                "expert",
                scatter_dimension=0,
                tiled=True,
            )
        )
    combined = jnp.concatenate(combined_parts, axis=-1)
    residual_out = (hidden_state.astype(jnp.float32) + combined.astype(jnp.float32)).astype(
        jnp.bfloat16
    )
    next_normed = rms_scale(residual_out, gain_next).astype(jnp.bfloat16)
    return (residual_out, next_normed)


def solution(mesh):
    placed = (
        P("expert", None, None, "dp"),
        P("dp", None),
        P(("dp", "expert"), None),
        P(),
        P(),
        P(),
        P(("dp", "expert"), None),
        P(("dp", "expert"), None),
        P(),
        P(),
        P("expert", "dp", None),
        P("expert", "dp", None),
    )
    return jax.shard_map(
        on_device_body,
        mesh=mesh,
        in_specs=placed,
        out_specs=(P(("dp", "expert"), None), P(("dp", "expert"), None)),
        check_vma=False,
    )
```

```python
import math

import jax
import jax.numpy as jnp
from jax import lax
from jax.sharding import PartitionSpec as P


CAP_UNIT = 8
CAP_MOST = 32


def rms_scale(values, gain):
    widened = values.astype(jnp.float32)
    return widened * lax.rsqrt(jnp.mean(widened * widened, axis=-1, keepdims=True) + 1e-06) * gain


def route_rows(logits, w_router, expert_ids, replica_pick, slot_expert, cap_blocks, cap_unit):
    blocks, row_count, topk_all = expert_ids.shape
    experts_all = w_router.shape[1]
    slots_all = slot_expert.shape[0]
    logits = logits.reshape(blocks, row_count, experts_all)
    expert_axis = jnp.arange(experts_all)
    one_hot = expert_ids[..., None] == expert_axis
    chosen = jnp.sum(jnp.where(one_hot, logits[:, :, None, :], jnp.float32(0.0)), axis=-1)
    raised = jnp.exp(chosen)
    gates = raised / jnp.sum(raised, axis=-1, keepdims=True)
    holder = (slot_expert[None, :] == expert_axis[:, None]).astype(jnp.int32)
    rep_count = jnp.sum(holder, axis=1)
    earlier = jnp.cumsum(holder, axis=1) - holder
    slot_rank = jnp.sum(earlier * holder, axis=0)
    count_of = jnp.sum(jnp.where(one_hot, rep_count, 0), axis=-1)
    replica = replica_pick % count_of
    slot_axis = jnp.arange(slots_all)
    matched = (slot_expert == expert_ids[..., None]) & (slot_rank == replica[..., None])
    target_slot = jnp.sum(jnp.where(matched, slot_axis, 0), axis=-1)
    flat_count = row_count * topk_all
    selected = matched.reshape(blocks, flat_count, slots_all)
    flat_axis = lax.optimization_barrier(jnp.arange(flat_count))
    lower = (flat_axis[:, None] > flat_axis[None, :]).astype(jnp.bfloat16)
    before = jnp.einsum(
        "ij,bjs->bis", lower, selected.astype(jnp.bfloat16), preferred_element_type=jnp.float32
    )
    position = (
        jnp.sum(jnp.where(selected, before, jnp.float32(0.0)), axis=-1)
        .astype(jnp.int32)
        .reshape(blocks, row_count, topk_all)
    )
    capacity = (
        jnp.sum(jnp.where(target_slot[..., None] == slot_axis, cap_blocks, 0), axis=-1) * cap_unit
    )
    retained = position < capacity
    return (gates, target_slot, position, retained)


def unit_plan(slot_local, n_dp, hidden_units):
    full = slot_local // n_dp
    rest = slot_local - full * n_dp
    chunks = n_dp // math.gcd(rest, n_dp) if rest else 1
    halves = rest * chunks // n_dp
    chunk_width = hidden_units // chunks
    owned_full = [[o * full + j for j in range(full)] for o in range(n_dp)]
    if halves == 1 and rest * chunks == n_dp:
        owned_part = [[(full * n_dp + o % rest, o // rest)] for o in range(n_dp)]
    else:
        owned_part = [
            [(full * n_dp + (o * halves + i) // chunks, (o * halves + i) % chunks)
             for i in range(halves)]
            for o in range(n_dp)
        ]
    return full, halves, chunks, chunk_width, owned_full, owned_part


def on_device_body(
    context,
    w_proj,
    residual,
    gain_first,
    gain_next,
    w_router,
    expert_ids,
    replica_pick,
    slot_expert,
    cap_blocks,
    w_in,
    w_out,
):
    tok_rows, model_width = residual.shape
    topk_all = expert_ids.shape[1]
    slot_local, d_local, _ = w_in.shape
    hidden_units = w_in.shape[2] // 2
    ff_local = w_out.shape[1]
    n_dp = lax.axis_size("dp")
    n_exp = lax.axis_size("expert")
    dp_at = lax.axis_index("dp")
    exp_at = lax.axis_index("expert")
    full, halves, chunks, chunk_width, owned_full, owned_part = unit_plan(
        slot_local, n_dp, hidden_units
    )
    sources_per_chunk = chunk_width // ff_local
    rest = slot_local - full * n_dp
    paired = (
        halves == 1 and rest * chunks == n_dp and chunk_width == rest * ff_local
    )
    lane_width = 2 * chunk_width if (ff_local * model_width) % (2 * chunk_width) == 0 else 128

    def as_rows(piece):
        return piece.reshape(-1, lane_width)

    weight_parts = []
    for o in range(n_dp):
        pieces = []
        for s in owned_full[o]:
            pieces += [as_rows(w_in[s]), as_rows(w_out[s])]
        for s, c in owned_part[o]:
            lo = c * chunk_width
            pieces += [
                as_rows(w_in[s, :, lo:lo + chunk_width]),
                as_rows(w_in[s, :, hidden_units + lo:hidden_units + lo + chunk_width]),
            ]
            if not paired:
                pieces.append(as_rows(w_out[s]))
        weight_parts.append(jnp.concatenate(pieces, axis=0))
    weight_send = jnp.stack(weight_parts)
    weight_recv = lax.all_to_all(weight_send, "dp", 0, 0, tiled=True)
    offset = 0


    def take(shape):
        nonlocal offset
        count = math.prod(shape) // lane_width
        piece = weight_recv[:, offset:offset + count].reshape((n_dp,) + shape)
        offset += count
        return piece

    full_in, full_out, part_in, part_out = [], [], [], []
    for _ in range(full):
        full_in.append(take((d_local, 2 * hidden_units)).reshape(n_dp * d_local, 2 * hidden_units))
        full_out.append(take((ff_local, model_width)).reshape(n_dp * ff_local, model_width))
    for _ in range(halves):
        gate_in = take((d_local, chunk_width))
        up_in = take((d_local, chunk_width))
        part_in.append(
            jnp.concatenate([gate_in, up_in], axis=-1).reshape(n_dp * d_local, 2 * chunk_width)
        )
        if not paired:
            part_out.append(take((ff_local, model_width)))
    if paired:
        group_at = dp_at % rest
        held = [lax.dynamic_index_in_dim(w_out, full * n_dp + group_at, 0, keepdims=False)]
        for k in range(1, rest):
            sent = lax.dynamic_index_in_dim(
                w_out, full * n_dp + (group_at + rest - k) % rest, 0, keepdims=False
            )
            pairs = [
                (base + (p + k) % rest, base + p)
                for base in range(0, n_dp, rest)
                for p in range(rest)
            ]
            held.append(lax.ppermute(sent, "dp", pairs))
        part_out.append(
            jnp.roll(jnp.stack(held), group_at, axis=0).reshape(chunk_width, model_width)
        )

    ids_all = lax.all_gather(
        jnp.concatenate([expert_ids, replica_pick], axis=1), "expert", axis=0, tiled=True
    ).reshape(n_exp, tok_rows, 2 * topk_all)

    flat_context = context.reshape(-1, context.shape[3])
    head_parts = jnp.dot(flat_context, w_proj, preferred_element_type=jnp.float32)
    head_parts = lax.all_to_all(
        head_parts.reshape(n_dp, tok_rows, model_width), "dp", 0, 0, tiled=True
    )
    attended = jnp.sum(head_parts, axis=0)
    hidden_state = (residual.astype(jnp.float32) + attended.astype(jnp.float32)).astype(
        jnp.bfloat16
    )
    normed = rms_scale(hidden_state, gain_first).astype(jnp.bfloat16)

    normed_all = lax.all_gather(normed, "expert", axis=0, tiled=True)
    logits = jnp.dot(normed_all, w_router, preferred_element_type=jnp.float32)
    gates, target_slot, position, retained = route_rows(
        logits,
        w_router,
        ids_all[:, :, :topk_all],
        ids_all[:, :, topk_all:],
        slot_expert,
        cap_blocks,
        CAP_UNIT,
    )
    here = retained & (target_slot // slot_local == exp_at)
    local = jnp.where(here, (target_slot % slot_local) * CAP_MOST + position, -1)
    hit = local[..., None] == jnp.arange(slot_local * CAP_MOST)
    pick = jnp.any(hit, axis=2).astype(jnp.bfloat16)
    weight = jnp.sum(jnp.where(hit, gates[..., None], jnp.float32(0.0)), axis=2)
    slot_in = jnp.einsum(
        "btr,btd->brd",
        pick,
        normed_all.reshape(n_exp, tok_rows, model_width),
        preferred_element_type=jnp.float32,
    ).astype(jnp.bfloat16)
    slot_in = slot_in.reshape(n_exp, slot_local, CAP_MOST, model_width)

    x_parts = []
    for o in range(n_dp):
        x_parts.append(
            jnp.stack([slot_in[:, s] for s in owned_full[o]] + [slot_in[:, s] for s, _ in owned_part[o]])
        )
    x_recv = lax.all_to_all(jnp.stack(x_parts), "dp", 0, 0, tiled=True)

    unit_rows = n_dp * n_exp * CAP_MOST

    def activate(rows, w_up, width):
        gate_up = jnp.dot(rows, w_up, preferred_element_type=jnp.float32)
        return (jax.nn.silu(gate_up[:, :width]) * gate_up[:, width:]).astype(jnp.bfloat16)

    acts, downs = [], []
    for j in range(full):
        rows = x_recv[:, j].reshape(unit_rows, model_width)
        acts.append(activate(rows, full_in[j], hidden_units))
        downs.append(full_out[j])
    for i in range(halves):
        rows = x_recv[:, full + i].reshape(unit_rows, model_width)
        if paired:
            w_down = part_out[i]
        else:
            chunk_at = (dp_at * halves + i) % chunks
            w_down = lax.dynamic_slice_in_dim(
                part_out[i], chunk_at * sources_per_chunk, sources_per_chunk, axis=0
            ).reshape(chunk_width, model_width)
        acts.append(activate(rows, part_in[i], chunk_width))
        downs.append(w_down)

    def returned_piece(cols):
        outs = [
            jnp.dot(act, down[:, cols], preferred_element_type=jnp.float32)
            .astype(jnp.bfloat16)
            .reshape(n_dp, n_exp, CAP_MOST, -1)
            for act, down in zip(acts, downs)
        ]
        return jnp.stack(outs, axis=1)

    weight_hi = weight.astype(jnp.bfloat16)
    weight_lo = (weight - weight_hi.astype(jnp.float32)).astype(jnp.bfloat16)
    halves_d = 1
    piece_width = model_width // halves_d
    combined_parts = []
    for h in range(halves_d):
        cols = slice(h * piece_width, (h + 1) * piece_width)
        y_recv = lax.all_to_all(returned_piece(cols), "dp", 0, 0, tiled=True)
        slot_out = [None] * slot_local
        for o in range(n_dp):
            for j, s in enumerate(owned_full[o]):
                slot_out[s] = y_recv[o, j]
            for i, (s, _) in enumerate(owned_part[o]):
                part = y_recv[o, full + i].astype(jnp.float32)
                slot_out[s] = part if slot_out[s] is None else slot_out[s] + part
        slot_out = [part.astype(jnp.bfloat16) for part in slot_out]
        expert_out = jnp.stack(slot_out, axis=1).reshape(
            n_exp, slot_local * CAP_MOST, piece_width
        )
        partial = jnp.einsum(
            "btr,brd->btd", weight_hi, expert_out, preferred_element_type=jnp.float32
        ) + jnp.einsum("btr,brd->btd", weight_lo, expert_out, preferred_element_type=jnp.float32)
        combined_parts.append(
            lax.psum_scatter(
                partial.reshape(n_exp * tok_rows, piece_width).astype(jnp.bfloat16),
                "expert",
                scatter_dimension=0,
                tiled=True,
            )
        )
    combined = jnp.concatenate(combined_parts, axis=-1)
    residual_out = (hidden_state.astype(jnp.float32) + combined.astype(jnp.float32)).astype(
        jnp.bfloat16
    )
    next_normed = rms_scale(residual_out, gain_next).astype(jnp.bfloat16)
    return (residual_out, next_normed)


def solution(mesh):
    placed = (
        P("expert", None, None, "dp"),
        P("dp", None),
        P(("dp", "expert"), None),
        P(),
        P(),
        P(),
        P(("dp", "expert"), None),
        P(("dp", "expert"), None),
        P(),
        P(),
        P("expert", "dp", None),
        P("expert", "dp", None),
    )
    return jax.shard_map(
        on_device_body,
        mesh=mesh,
        in_specs=placed,
        out_specs=(P(("dp", "expert"), None), P(("dp", "expert"), None)),
        check_vma=False,
    )
```
